256 devices in a mesh: clip: 4 (over z_hi, core), fsdp: 64 (over y, z_lo, x).
Axes of the slice: x: 4, y: 4, z: 8 (z_hi: 2, z_lo: 4; z = z_hi * 4 + z_lo), core: 2. Of those that a mesh axis runs over, the one named last changes fastest.
Arguments:
- span_queries: bfloat16 [64, 512, 2560], P('fsdp', None, 'clip'), may hold values from -20 to 20
- span_keys: bfloat16 [64, 512, 2560], P('fsdp', None, 'clip'), may hold values from -12 to 12
- span_values: bfloat16 [64, 512, 2560], P('fsdp', None, 'clip'), may hold values from -6 to 6
- cache_keys: bfloat16 [128, 512, 2560], P(None, 'fsdp', 'clip'), may hold values from -6 to 6
- cache_values: bfloat16 [128, 512, 2560], P(None, 'fsdp', 'clip'), may hold values from -6 to 6
- page_table: int32 [128], replicated, may hold values from 0 to 127, each once
- frame_lists: int32 [64, 6], replicated, may hold values from 0 to 15, as said below
- list_counts: int32 [64], replicated, may hold values from 1 to 6, as said below
- out_weight: bfloat16 [2560, 5120], P('clip', 'fsdp'), may hold values from -1 to 1
Outputs:
- projected: bfloat16 [64, 512, 5120], P('fsdp', 'clip')
The draws below stay inside these ranges and needn't reach their ends.
Inputs may be any that keep to these rules, and one draw needn't show every extreme that they name: `frame_lists`: each row holds 6 different cached frames; a frame attends to the first list_counts of them. `list_counts`: the counts of frames 2 * i and 2 * i + 1 sum to exactly 7; some frame attends to exactly 6. `page_table`: every block number once.
All inputs are finite; a program needn't handle non-finite values.
Results may differ from the reference program's by a relative error of at most 0.017.
Values may be sent and summed in bfloat16 or wider, within the bound.
No kernel may reach another device: no remote copies, remote signals or barrier semaphores. Data moves between devices by JAX's collectives and lax.ppermute only.
A program may use at most 128 MiB of HBM per device.

```python
import math
import jax
import jax.numpy as jnp
from jax import lax

D = 5120
HD = 128
HEADS = 20
FT = 512
CF = 8
NC = 16
MAXL = 6
FRAMES = 64
BLOCKS = 128
N_CLIP = 4


def draw_together(key):
    pair_key = jax.random.fold_in(key, 101)
    subkeys = jax.random.split(pair_key, 2)
    array_shape = (FRAMES, FT, HEADS * HD)
    query_draw = 1.5 * jax.random.truncated_normal(subkeys[0], -4.0, 4.0, array_shape, jnp.float32)
    key_draw = jax.random.truncated_normal(subkeys[1], -4.0, 4.0, array_shape, jnp.float32)
    return (query_draw, key_draw)


def draw_span_queries(key, part):
    return draw_together(key)[0].astype(jnp.bfloat16)


def draw_span_keys(key, part):
    return draw_together(key)[1].astype(jnp.bfloat16)


def draw_frame_lists(key, part):
    list_key = jax.random.fold_in(key, 11)
    ranking_scores = jax.random.randint(list_key, (FRAMES, NC), 0, 1 << 20) * NC + jnp.arange(NC, dtype=jnp.int32)[None, :]
    ranking = jnp.argsort(ranking_scores, axis=1, stable=True).astype(jnp.int32)
    return ranking[:, :MAXL]


def draw_list_counts(key, part):
    subkeys = jax.random.split(jax.random.fold_in(key, 23), 2)
    pairs = FRAMES // 2
    first_counts = jax.random.randint(subkeys[0], (pairs,), 1, MAXL + 1)
    forced_pair = jax.random.randint(subkeys[1], (), 0, pairs)
    first_counts = jnp.where(jnp.arange(pairs, dtype=jnp.int32) == forced_pair, MAXL, first_counts)
    second_counts = MAXL + 1 - first_counts
    return jnp.stack([first_counts, second_counts], axis=1).reshape(FRAMES).astype(jnp.int32)


def steps_of(own_key, dims, cuts, low, high):
    loudness = 1.0
    for axis_at, shards_of in cuts:
        heights = jax.random.uniform(jax.random.fold_in(jax.random.fold_in(own_key, 6), axis_at), (shards_of,), jnp.float32, low / len(cuts), high / len(cuts))
        loudness = loudness * jnp.repeat(jnp.exp(heights), dims[axis_at] // shards_of).reshape((-1,) + (1,) * (len(dims) - 1 - axis_at))
    return loudness


def bell_draw(key, extent, width, most, cuts=(), kind=jnp.bfloat16):
    values = width * jax.random.normal(key, extent, jnp.float32)
    if cuts:
        values = values * steps_of(key, extent, cuts, -0.22, 0.18)
    return jnp.clip(values, -most, most).astype(kind)


def setup_inputs(seed: int = 0) -> dict:
    key_of = jax.random.split(jax.random.key(seed), 10)
    return {
        "span_queries": draw_span_queries(jax.random.fold_in(key_of[9], 71), 0),
        "span_keys": draw_span_keys(jax.random.fold_in(key_of[9], 71), 0),
        "span_values": bell_draw(key_of[2], (FRAMES, FT, HEADS * HD), 1.0, 6.0, ((0, 64), (2, 4))),
        "cache_keys": bell_draw(key_of[3], (BLOCKS, FT, HEADS * HD), 1.0, 6.0, ((1, 64), (2, 4))),
        "cache_values": bell_draw(key_of[4], (BLOCKS, FT, HEADS * HD), 1.0, 6.0, ((1, 64), (2, 4))),
        "page_table": jax.random.permutation(key_of[5], BLOCKS).astype(jnp.int32),
        "frame_lists": draw_frame_lists(jax.random.fold_in(key_of[9], 71), 0),
        "list_counts": draw_list_counts(jax.random.fold_in(key_of[9], 71), 0),
        "out_weight": bell_draw(key_of[8], (HEADS * HD, D), (HEADS * HD // 64) ** -0.5, 1.0, ((0, 4), (1, 64))),
    }


neg_fill = -1e+30

def one_frame(frame_item, cache_keys, cache_values, page_table, out_weight):
    query_rows, key_rows, value_rows, listed, item_count, frame_index = frame_item
    clip_index = frame_index // CF
    blocks = page_table[(clip_index * NC + listed).astype(jnp.int32)].astype(jnp.int32)
    key_set = jnp.concatenate([key_rows[None], cache_keys[blocks]], axis=0).reshape((MAXL + 1) * FT, HEADS, HD)
    value_set = jnp.concatenate([value_rows[None], cache_values[blocks]], axis=0).reshape((MAXL + 1) * FT, HEADS, HD)
    live_slots = jnp.arange(MAXL + 1, dtype=jnp.int32) <= item_count
    live_keys = jnp.repeat(live_slots, FT)
    scores = jnp.einsum('qhd,khd->qhk', query_rows.reshape(FT, HEADS, HD).astype(jnp.float32), key_set.astype(jnp.float32)) * (1.0 / math.sqrt(HD))
    scores = jnp.where(live_keys[None, None, :], scores, neg_fill)
    top_score = lax.optimization_barrier(jnp.max(scores, axis=2, keepdims=True))
    weights = jnp.exp(scores - top_score)
    denominators = lax.optimization_barrier(jnp.sum(weights, axis=2))
    rounded = lax.optimization_barrier(weights.astype(jnp.bfloat16)).astype(jnp.float32)
    summed = jnp.einsum('qhk,khd->qhd', rounded, value_set.astype(jnp.float32))
    attended = (summed / denominators[:, :, None]).reshape(FT, HEADS * HD).astype(jnp.bfloat16)
    group_width = HEADS // N_CLIP * HD
    combined = jnp.zeros((FT, D), jnp.float32)
    for group_index in range(N_CLIP):
        lower = group_index * group_width
        partial_value = jnp.dot(attended[:, lower:lower + group_width], out_weight[lower:lower + group_width], preferred_element_type=jnp.float32)
        combined = combined + lax.optimization_barrier(partial_value.astype(jnp.bfloat16)).astype(jnp.float32)
    return combined.astype(jnp.bfloat16)

def reference(span_queries, span_keys, span_values, cache_keys, cache_values, page_table, frame_lists, list_counts, out_weight):
    frame_numbers = jnp.arange(FRAMES, dtype=jnp.int32)

    def per_frame(frame_item):
        return one_frame(frame_item, cache_keys, cache_values, page_table, out_weight)
    return lax.map(per_frame, (span_queries, span_keys, span_values, frame_lists, list_counts, frame_numbers))
```

```python
import math

import jax
import jax.numpy as jnp
import numpy as np
from jax import lax
from jax.sharding import Mesh
from jax.sharding import PartitionSpec as P

HD = 128
CF = 8
NC = 16

FRAME_AXES = ("y", "zl", "x")

neg_fill = -1e30


def empty_state(tokens_here, heads_here):
    return (
        jnp.full((tokens_here, heads_here), neg_fill, jnp.float32),
        jnp.zeros((tokens_here, heads_here), jnp.float32),
        jnp.zeros((tokens_here, heads_here, HD), jnp.float32),
    )


def absorb(carried, query_block, key_block, value_block):
    running_max, running_sum, running_out = carried
    scores = jnp.einsum(
        "qhd,khd->qhk", query_block, key_block, preferred_element_type=jnp.float32
    ) * (1.0 / math.sqrt(HD))
    new_max = jnp.maximum(running_max, jnp.max(scores, axis=2))
    shrink = jnp.exp(running_max - new_max)
    weights = jnp.exp(scores - new_max[:, :, None])
    running_sum = running_sum * shrink + jnp.sum(weights, axis=2)
    running_out = running_out * shrink[:, :, None] + jnp.einsum(
        "qhk,khd->qhd",
        weights.astype(jnp.bfloat16),
        value_block,
        preferred_element_type=jnp.float32,
    )
    return (new_max, running_sum, running_out)


def pair_schedule(frames, half_slots, page_table, frame_lists, list_counts):
    dest = jnp.arange(frames, dtype=jnp.int32)[:, None]
    slot = jnp.arange(half_slots, dtype=jnp.int32)[None, :]
    even = dest - dest % 2
    global_half = (dest % 2) * half_slots + slot
    combined = global_half // 2
    row_half = global_half % 2
    even_count = list_counts[even]
    for_even = combined < even_count
    listed_even = frame_lists[even, jnp.minimum(combined, frame_lists.shape[1] - 1)]
    listed_odd = frame_lists[even + 1, jnp.clip(combined - even_count, 0, frame_lists.shape[1] - 1)]
    listed = jnp.where(for_even, listed_even, listed_odd)
    blocks = page_table[(even // CF) * NC + listed]
    return blocks, row_half, for_even


def local(
    span_queries,
    span_keys,
    span_values,
    cache_keys,
    cache_values,
    page_table,
    frame_lists,
    list_counts,
    out_weight,
):
    frames = lax.axis_size(FRAME_AXES)
    own_frame = lax.axis_index(FRAME_AXES)
    tokens_here = span_queries.shape[1]
    row_width = span_queries.shape[2]
    heads_here = row_width // HD
    blocks_total, rows_here, _ = cache_keys.shape
    half_rows = rows_here // 2
    half_slots = frame_lists.shape[1] + 1
    own_queries = span_queries[0].reshape(tokens_here, heads_here, HD)
    own_keys = span_keys[0].reshape(tokens_here, heads_here, HD)
    own_values = span_values[0].reshape(tokens_here, heads_here, HD)

    blocks, row_half, for_even = pair_schedule(
        frames, half_slots, page_table, frame_lists, list_counts
    )
    split_keys = cache_keys.reshape(blocks_total, 2, half_rows, row_width)
    split_values = cache_values.reshape(blocks_total, 2, half_rows, row_width)
    sent = jnp.stack(
        [split_keys[blocks, row_half], split_values[blocks, row_half]], axis=1
    )
    sent = sent.reshape(frames, -1, 128)
    arrived = lax.all_to_all(sent, FRAME_AXES, split_axis=0, concat_axis=0, tiled=True)
    arrived = arrived.reshape(frames, 2, half_slots, half_rows, heads_here, HD)
    arrived = arrived.transpose(1, 2, 0, 3, 4, 5).reshape(
        2, half_slots, frames * half_rows, heads_here, HD
    )
    arrived_keys = arrived[0]
    arrived_values = arrived[1]

    swap = [(i, i ^ 1) for i in range(lax.axis_size("x"))]
    partner_queries = lax.ppermute(own_queries, "x", swap)
    is_even = own_frame % 2 == 0
    mine = for_even[own_frame] == is_even

    own_state = absorb(
        empty_state(tokens_here, heads_here), own_queries, own_keys, own_values
    )
    other_state = empty_state(tokens_here, heads_here)
    def advance(slot, states):
        key_block = arrived_keys[slot]
        value_block = arrived_values[slot]

        def take_own(states):
            return (absorb(states[0], own_queries, key_block, value_block), states[1])

        def take_other(states):
            return (states[0], absorb(states[1], partner_queries, key_block, value_block))

        return lax.cond(mine[slot], take_own, take_other, states)

    own_state, other_state = lax.fori_loop(
        0, half_slots, advance, (own_state, other_state)
    )

    got_max, got_sum, got_out = lax.ppermute(other_state, "x", swap)
    own_max, own_sum, own_out = own_state
    top = jnp.maximum(own_max, got_max)
    own_scale = jnp.exp(own_max - top)
    got_scale = jnp.exp(got_max - top)
    total_sum = own_sum * own_scale + got_sum * got_scale
    total_out = own_out * own_scale[:, :, None] + got_out * got_scale[:, :, None]
    attended = (
        (total_out / total_sum[:, :, None]).astype(jnp.bfloat16).reshape(tokens_here, row_width)
    )
    weight = out_weight
    for axis in reversed(FRAME_AXES):
        weight = lax.all_gather(weight, axis, axis=1, tiled=True)
    partial_value = jnp.dot(attended, weight, preferred_element_type=jnp.float32)
    own_rows = lax.psum_scatter(
        partial_value.astype(jnp.bfloat16), "clip", scatter_dimension=0, tiled=True
    )
    return own_rows[None]


def solution(mesh):
    frames = mesh.shape["fsdp"]
    fine = Mesh(
        np.asarray(mesh.devices).reshape(mesh.shape["clip"], frames // 16, 4, 4),
        ("clip",) + FRAME_AXES,
    )
    in_specs = (
        P(FRAME_AXES, None, "clip"),
        P(FRAME_AXES, None, "clip"),
        P(FRAME_AXES, None, "clip"),
        P(None, FRAME_AXES, "clip"),
        P(None, FRAME_AXES, "clip"),
        P(),
        P(),
        P(),
        P("clip", FRAME_AXES),
    )
    out_specs = P(FRAME_AXES, "clip", None)
    return jax.shard_map(local, mesh=fine, in_specs=in_specs, out_specs=out_specs, check_vma=False)
```

```python
import math

import jax
import jax.numpy as jnp
import numpy as np
from jax import lax
from jax.sharding import Mesh
from jax.sharding import PartitionSpec as P

HD = 128
CF = 8
NC = 16

FRAME_AXES = ("y", "zl", "x")

neg_fill = -1e30


def empty_state(tokens_here, heads_here):
    return (
        jnp.full((tokens_here, heads_here), neg_fill, jnp.float32),
        jnp.zeros((tokens_here, heads_here), jnp.float32),
        jnp.zeros((tokens_here, heads_here, HD), jnp.float32),
    )


def absorb(carried, query_block, key_block, value_block):
    running_max, running_sum, running_out = carried
    scores = jnp.einsum(
        "qhd,khd->qhk", query_block, key_block, preferred_element_type=jnp.float32
    ) * (1.0 / math.sqrt(HD))
    new_max = jnp.maximum(running_max, jnp.max(scores, axis=2))
    shrink = jnp.exp(running_max - new_max)
    weights = jnp.exp(scores - new_max[:, :, None])
    running_sum = running_sum * shrink + jnp.sum(weights, axis=2)
    running_out = running_out * shrink[:, :, None] + jnp.einsum(
        "qhk,khd->qhd",
        weights.astype(jnp.bfloat16),
        value_block,
        preferred_element_type=jnp.float32,
    )
    return (new_max, running_sum, running_out)


def lookup(values_table, positions):
    table_width = values_table.shape[0]
    matches = positions[..., None] == jnp.arange(table_width, dtype=jnp.int32)
    return jnp.sum(jnp.where(matches, values_table, 0), axis=-1)


def pair_schedule(frames, slots, page_table, frame_lists, list_counts):
    max_slots = frame_lists.shape[1]
    dest = jnp.arange(frames, dtype=jnp.int32)[:, None]
    slot = jnp.arange(slots, dtype=jnp.int32)[None, :]
    even = dest - dest % 2
    combined = jnp.minimum((dest % 2) * slots + slot, max_slots)
    even_count = lookup(list_counts, even)
    for_even = combined < even_count
    listed_even = lookup(frame_lists.reshape(-1), even * max_slots + jnp.minimum(combined, max_slots - 1))
    listed_odd = lookup(
        frame_lists.reshape(-1),
        (even + 1) * max_slots + jnp.clip(combined - even_count, 0, max_slots - 1),
    )
    listed = jnp.where(for_even, listed_even, listed_odd)
    return lookup(page_table, (even // CF) * NC + listed)


def local(
    span_queries,
    span_keys,
    span_values,
    cache_keys,
    cache_values,
    page_table,
    frame_lists,
    list_counts,
    out_weight,
):
    frames = lax.axis_size(FRAME_AXES)
    own_frame = lax.axis_index(FRAME_AXES)
    tokens_here = span_queries.shape[1]
    row_width = span_queries.shape[2]
    heads_here = row_width // HD
    max_slots = frame_lists.shape[1]
    pair_blocks = max_slots + 1
    slots = (pair_blocks + 1) // 2
    own_queries = span_queries[0].reshape(tokens_here, heads_here, HD)
    own_keys = span_keys[0].reshape(tokens_here, heads_here, HD)
    own_values = span_values[0].reshape(tokens_here, heads_here, HD)

    weight = lax.all_gather(out_weight, ("zl", "x"), axis=1, tiled=True)
    weight = lax.all_gather(weight, "y", axis=1, tiled=True)

    blocks = pair_schedule(frames, slots, page_table, frame_lists, list_counts).T
    sent = jnp.stack([cache_keys[blocks], cache_values[blocks]], axis=0)
    arrived = lax.all_to_all(sent, FRAME_AXES, split_axis=2, concat_axis=2, tiled=True)
    arrived = arrived.reshape(2, slots, tokens_here, heads_here, HD)
    arrived_keys = arrived[0]
    arrived_values = arrived[1]

    swap = [(i, i ^ 1) for i in range(lax.axis_size("x"))]
    partner_queries = lax.ppermute(own_queries, "x", swap)
    odd = own_frame % 2
    even_count = lookup(list_counts, own_frame - odd)
    other_count = jnp.where(
        odd == 0, jnp.maximum(0, slots - even_count), jnp.maximum(0, even_count - slots)
    )
    mine_count = jnp.where(
        odd == 0, jnp.minimum(even_count, slots), pair_blocks - jnp.maximum(even_count, slots)
    )

    def slot_of(step):
        return jnp.where(odd == 0, slots - 1 - step, step)

    def advance_other(step, state):
        slot = slot_of(step)
        return absorb(state, partner_queries, arrived_keys[slot], arrived_values[slot])

    def advance_own(step, state):
        slot = slot_of(step)
        return absorb(state, own_queries, arrived_keys[slot], arrived_values[slot])

    other_state = lax.fori_loop(
        0, other_count, advance_other, empty_state(tokens_here, heads_here)
    )
    got_max, got_sum, got_out = lax.ppermute(other_state, "x", swap)
    own_state = absorb(
        empty_state(tokens_here, heads_here), own_queries, own_keys, own_values
    )
    own_state = lax.fori_loop(other_count, other_count + mine_count, advance_own, own_state)

    own_max, own_sum, own_out = own_state
    top = jnp.maximum(own_max, got_max)
    own_scale = jnp.exp(own_max - top)
    got_scale = jnp.exp(got_max - top)
    total_sum = own_sum * own_scale + got_sum * got_scale
    total_out = own_out * own_scale[:, :, None] + got_out * got_scale[:, :, None]
    attended = (
        (total_out / total_sum[:, :, None]).astype(jnp.bfloat16).reshape(tokens_here, row_width)
    )
    partial_value = jnp.dot(attended, weight, preferred_element_type=jnp.float32)
    own_rows = lax.psum_scatter(
        partial_value.astype(jnp.bfloat16), "clip", scatter_dimension=0, tiled=True
    )
    return own_rows[None]


def solution(mesh):
    frames = mesh.shape["fsdp"]
    fine = Mesh(
        np.asarray(mesh.devices).reshape(mesh.shape["clip"], frames // 16, 4, 4),
        ("clip",) + FRAME_AXES,
    )
    in_specs = (
        P(FRAME_AXES, None, "clip"),
        P(FRAME_AXES, None, "clip"),
        P(FRAME_AXES, None, "clip"),
        P(None, FRAME_AXES, "clip"),
        P(None, FRAME_AXES, "clip"),
        P(),
        P(),
        P(),
        P("clip", FRAME_AXES),
    )
    out_specs = P(FRAME_AXES, "clip", None)
    return jax.shard_map(local, mesh=fine, in_specs=in_specs, out_specs=out_specs, check_vma=False)
```

```python
import math

import jax
import jax.numpy as jnp
import numpy as np
from jax import lax
from jax.experimental import pallas as pl
from jax.experimental.pallas import tpu as pltpu
from jax.sharding import Mesh
from jax.sharding import PartitionSpec as P

HD = 128
CF = 8
NC = 16

FRAME_AXES = ("y", "zl", "x")

neg_fill = -1e30


def attend_kernel(order_ref, count_ref, q_ref, k_ref, v_ref, *rest, with_own):
    if with_own:
        own_k_ref, own_v_ref, o_ref, m_ref, l_ref = rest
    else:
        o_ref, m_ref, l_ref = rest
    step = pl.program_id(1)
    first = 1 if with_own else 0

    @pl.when(step == 0)
    def _init():
        m_ref[...] = jnp.full(m_ref.shape, neg_fill, jnp.float32)
        l_ref[...] = jnp.zeros(l_ref.shape, jnp.float32)
        o_ref[...] = jnp.zeros(o_ref.shape, jnp.float32)

    def absorb(key_block, value_block):
        scores = lax.dot_general(
            q_ref[...], key_block, (((1,), (1,)), ((), ())),
            preferred_element_type=jnp.float32,
        ) * (1.0 / math.sqrt(HD))
        running_max = m_ref[:, :1]
        new_max = jnp.maximum(running_max, jnp.max(scores, axis=1, keepdims=True))
        shrink = jnp.exp(running_max - new_max)
        weights = jnp.exp(scores - new_max)
        l_ref[...] = l_ref[...] * shrink + jnp.sum(weights, axis=1, keepdims=True)
        o_ref[...] = o_ref[...] * shrink + jnp.dot(
            weights.astype(jnp.bfloat16), value_block, preferred_element_type=jnp.float32
        )
        m_ref[...] = jnp.broadcast_to(new_max, m_ref.shape)

    if with_own:
        @pl.when(step == 0)
        def _own():
            absorb(own_k_ref[...], own_v_ref[...])

    @pl.when((step >= first) & (step - first < count_ref[0]))
    def _slot():
        absorb(k_ref[0, 0], v_ref[0, 0])


def attend(queries, arrived, order, count, own_keys=None, own_values=None):
    tokens, width = queries.shape
    slots = arrived.shape[1]
    heads = width // HD
    with_own = own_keys is not None
    first = 1 if with_own else 0
    steps = slots + first

    def slot_at(s, order_ref, count_ref):
        visit = jnp.clip(s - first, 0, jnp.maximum(count_ref[0] - 1, 0))
        return order_ref[visit]

    q_spec = pl.BlockSpec((tokens, HD), lambda h, s, o, c: (0, h))
    k_spec = pl.BlockSpec((1, 1, tokens, HD), lambda h, s, o, c: (0, slot_at(s, o, c), 0, h))
    v_spec = pl.BlockSpec((1, 1, tokens, HD), lambda h, s, o, c: (1, slot_at(s, o, c), 0, h))
    in_specs = [q_spec, k_spec, v_spec]
    operands = [queries, arrived, arrived]
    if with_own:
        in_specs += [q_spec, q_spec]
        operands += [own_keys, own_values]
    out_spec = pl.BlockSpec((tokens, HD), lambda h, s, o, c: (0, h))
    state_shape = jax.ShapeDtypeStruct((tokens, width), jnp.float32)
    return pl.pallas_call(
        lambda *refs: attend_kernel(*refs, with_own=with_own),
        grid_spec=pltpu.PrefetchScalarGridSpec(
            num_scalar_prefetch=2,
            grid=(heads, steps),
            in_specs=in_specs,
            out_specs=[out_spec, out_spec, out_spec],
        ),
        out_shape=[state_shape, state_shape, state_shape],
        compiler_params=pltpu.CompilerParams(dimension_semantics=("arbitrary", "arbitrary")),
    )(order, count, *operands)


def lookup(values_table, positions):
    table_width = values_table.shape[0]
    matches = positions[..., None] == jnp.arange(table_width, dtype=jnp.int32)
    return jnp.sum(jnp.where(matches, values_table, 0), axis=-1)


def pair_schedule(frames, slots, page_table, frame_lists, list_counts):
    max_slots = frame_lists.shape[1]
    dest = jnp.arange(frames, dtype=jnp.int32)[:, None]
    slot = jnp.arange(slots, dtype=jnp.int32)[None, :]
    even = dest - dest % 2
    combined = jnp.minimum((dest % 2) * slots + slot, max_slots)
    even_count = lookup(list_counts, even)
    for_even = combined < even_count
    listed_even = lookup(frame_lists.reshape(-1), even * max_slots + jnp.minimum(combined, max_slots - 1))
    listed_odd = lookup(
        frame_lists.reshape(-1),
        (even + 1) * max_slots + jnp.clip(combined - even_count, 0, max_slots - 1),
    )
    listed = jnp.where(for_even, listed_even, listed_odd)
    return lookup(page_table, (even // CF) * NC + listed)


def local(
    span_queries,
    span_keys,
    span_values,
    cache_keys,
    cache_values,
    page_table,
    frame_lists,
    list_counts,
    out_weight,
):
    frames = lax.axis_size(FRAME_AXES)
    own_frame = lax.axis_index(FRAME_AXES)
    tokens_here = span_queries.shape[1]
    row_width = span_queries.shape[2]
    heads_here = row_width // HD
    max_slots = frame_lists.shape[1]
    pair_blocks = max_slots + 1
    slots = (pair_blocks + 1) // 2
    own_queries = span_queries[0]
    own_keys = span_keys[0]
    own_values = span_values[0]

    weight = lax.all_gather(out_weight, ("zl", "x"), axis=1, tiled=True)
    weight = lax.all_gather(weight, "y", axis=1, tiled=True)

    blocks = pair_schedule(frames, slots, page_table, frame_lists, list_counts).T
    sent = jnp.stack([cache_keys[blocks], cache_values[blocks]], axis=0)
    arrived = lax.all_to_all(sent, FRAME_AXES, split_axis=2, concat_axis=2, tiled=True)
    arrived = arrived.reshape(2, slots, tokens_here, row_width)

    swap = [(i, i ^ 1) for i in range(lax.axis_size("x"))]
    partner_queries = lax.ppermute(own_queries, "x", swap)
    odd = own_frame % 2
    even_count = lookup(list_counts, own_frame - odd)
    other_count = jnp.where(
        odd == 0, jnp.maximum(0, slots - even_count), jnp.maximum(0, even_count - slots)
    )
    mine_count = jnp.where(
        odd == 0, jnp.minimum(even_count, slots), pair_blocks - jnp.maximum(even_count, slots)
    )
    step = jnp.arange(slots, dtype=jnp.int32)
    visit = jnp.where(odd == 0, slots - 1 - step, step)
    own_visit = jnp.where(odd == 0, slots - 1 - jnp.minimum(step + other_count, slots - 1),
                          jnp.minimum(step + other_count, slots - 1))

    other_out, other_max, other_sum = attend(
        partner_queries, arrived, visit, other_count.reshape(1)
    )
    got_max, got_sum, got_out = lax.ppermute(
        (other_max[:, ::HD], other_sum[:, ::HD], other_out), "x", swap
    )
    own_out, own_max, own_sum = attend(
        own_queries, arrived, own_visit, mine_count.reshape(1), own_keys, own_values
    )
    got_max = jnp.repeat(got_max, HD, axis=1)
    got_sum = jnp.repeat(got_sum, HD, axis=1)
    top = jnp.maximum(own_max, got_max)
    own_scale = jnp.exp(own_max - top)
    got_scale = jnp.exp(got_max - top)
    total_sum = own_sum * own_scale + got_sum * got_scale
    total_out = own_out * own_scale + got_out * got_scale
    attended = (total_out / total_sum).astype(jnp.bfloat16)
    partial_value = jnp.dot(attended, weight, preferred_element_type=jnp.float32)
    own_rows = lax.psum_scatter(
        partial_value.astype(jnp.bfloat16), "clip", scatter_dimension=0, tiled=True
    )
    return own_rows[None]


def solution(mesh):
    frames = mesh.shape["fsdp"]
    fine = Mesh(
        np.asarray(mesh.devices).reshape(mesh.shape["clip"], frames // 16, 4, 4),
        ("clip",) + FRAME_AXES,
    )
    in_specs = (
        P(FRAME_AXES, None, "clip"),
        P(FRAME_AXES, None, "clip"),
        P(FRAME_AXES, None, "clip"),
        P(None, FRAME_AXES, "clip"),
        P(None, FRAME_AXES, "clip"),
        P(),
        P(),
        P(),
        P("clip", FRAME_AXES),
    )
    out_specs = P(FRAME_AXES, "clip", None)
    return jax.shard_map(local, mesh=fine, in_specs=in_specs, out_specs=out_specs, check_vma=False)
```

```python
import math

import jax
import jax.numpy as jnp
import numpy as np
from jax import lax
from jax.experimental import pallas as pl
from jax.experimental.pallas import tpu as pltpu
from jax.sharding import Mesh
from jax.sharding import PartitionSpec as P

HD = 128
CF = 8
NC = 16

FRAME_AXES = ("y", "zl", "x")

neg_fill = -1e30


def attend_kernel(order_ref, count_ref, q_ref, k_ref, v_ref, *rest, with_own):
    if with_own:
        own_k_ref, own_v_ref, o_ref, m_ref, l_ref = rest
    else:
        o_ref, m_ref, l_ref = rest
    step = pl.program_id(1)
    first = 1 if with_own else 0

    @pl.when(step == 0)
    def _init():
        m_ref[...] = jnp.full(m_ref.shape, neg_fill, jnp.float32)
        l_ref[...] = jnp.zeros(l_ref.shape, jnp.float32)
        o_ref[...] = jnp.zeros(o_ref.shape, jnp.float32)

    def absorb(key_block, value_block):
        scores = lax.dot_general(
            q_ref[...], key_block, (((1,), (1,)), ((), ())),
            preferred_element_type=jnp.float32,
        ) * (1.0 / math.sqrt(HD))
        running_max = m_ref[:, :1]
        new_max = jnp.maximum(running_max, jnp.max(scores, axis=1, keepdims=True))
        shrink = jnp.exp(running_max - new_max)
        weights = jnp.exp(scores - new_max)
        l_ref[...] = l_ref[...] * shrink + jnp.sum(weights, axis=1, keepdims=True)
        o_ref[...] = o_ref[...] * shrink + jnp.dot(
            weights.astype(jnp.bfloat16), value_block, preferred_element_type=jnp.float32
        )
        m_ref[...] = jnp.broadcast_to(new_max, m_ref.shape)

    if with_own:
        @pl.when(step == 0)
        def _own():
            absorb(own_k_ref[...], own_v_ref[...])

    @pl.when((step >= first) & (step - first < count_ref[0]))
    def _slot():
        absorb(k_ref[0, 0], v_ref[0, 0])


def attend(queries, arrived, order, count, own_keys=None, own_values=None):
    tokens, width = queries.shape
    slots = arrived.shape[1]
    heads = width // HD
    with_own = own_keys is not None
    first = 1 if with_own else 0
    steps = slots + first

    def slot_at(s, order_ref, count_ref):
        visit = jnp.clip(s - first, 0, jnp.maximum(count_ref[0] - 1, 0))
        return order_ref[visit]

    keys_each = arrived.shape[2]
    q_spec = pl.BlockSpec((tokens, HD), lambda h, s, o, c: (0, h))
    own_spec = pl.BlockSpec((keys_each, HD), lambda h, s, o, c: (0, h))
    k_spec = pl.BlockSpec((1, 1, keys_each, HD), lambda h, s, o, c: (0, slot_at(s, o, c), 0, h))
    v_spec = pl.BlockSpec((1, 1, keys_each, HD), lambda h, s, o, c: (1, slot_at(s, o, c), 0, h))
    in_specs = [q_spec, k_spec, v_spec]
    operands = [queries, arrived, arrived]
    if with_own:
        in_specs += [own_spec, own_spec]
        operands += [own_keys, own_values]
    out_spec = pl.BlockSpec((tokens, HD), lambda h, s, o, c: (0, h))
    state_shape = jax.ShapeDtypeStruct((tokens, width), jnp.float32)
    return pl.pallas_call(
        lambda *refs: attend_kernel(*refs, with_own=with_own),
        grid_spec=pltpu.PrefetchScalarGridSpec(
            num_scalar_prefetch=2,
            grid=(heads, steps),
            in_specs=in_specs,
            out_specs=[out_spec, out_spec, out_spec],
        ),
        out_shape=[state_shape, state_shape, state_shape],
        compiler_params=pltpu.CompilerParams(dimension_semantics=("arbitrary", "arbitrary")),
    )(order, count, *operands)


def lookup(values_table, positions):
    table_width = values_table.shape[0]
    matches = positions[..., None] == jnp.arange(table_width, dtype=jnp.int32)
    return jnp.sum(jnp.where(matches, values_table, 0), axis=-1)


def pair_schedule(frames, slots, page_table, frame_lists, list_counts):
    max_slots = frame_lists.shape[1]
    dest = jnp.arange(frames, dtype=jnp.int32)[:, None]
    slot = jnp.arange(slots, dtype=jnp.int32)[None, :]
    even = dest - dest % 2
    combined = jnp.minimum((dest % 2) * slots + slot, max_slots)
    even_count = lookup(list_counts, even)
    for_even = combined < even_count
    listed_even = lookup(frame_lists.reshape(-1), even * max_slots + jnp.minimum(combined, max_slots - 1))
    listed_odd = lookup(
        frame_lists.reshape(-1),
        (even + 1) * max_slots + jnp.clip(combined - even_count, 0, max_slots - 1),
    )
    listed = jnp.where(for_even, listed_even, listed_odd)
    return lookup(page_table, (even // CF) * NC + listed)


def local(
    span_queries,
    span_keys,
    span_values,
    cache_keys,
    cache_values,
    page_table,
    frame_lists,
    list_counts,
    out_weight,
):
    frames = lax.axis_size(FRAME_AXES)
    own_frame = lax.axis_index(FRAME_AXES)
    tokens_here = span_queries.shape[1]
    row_width = span_queries.shape[2]
    heads_here = row_width // HD
    max_slots = frame_lists.shape[1]
    pair_blocks = max_slots + 1
    slots = (pair_blocks + 1) // 2
    own_queries = span_queries[0]
    own_keys = span_keys[0]
    own_values = span_values[0]

    weight = lax.all_gather(out_weight, ("zl", "x"), axis=1, tiled=True)
    weight = lax.all_gather(weight, "y", axis=1, tiled=True)

    blocks = pair_schedule(frames, slots, page_table, frame_lists, list_counts).T
    sent = jnp.stack([cache_keys[blocks], cache_values[blocks]], axis=0)
    arrived = lax.all_to_all(sent, FRAME_AXES, split_axis=2, concat_axis=2, tiled=True)
    arrived = arrived.reshape(2, slots, tokens_here, row_width)

    swap = [(i, i ^ 1) for i in range(lax.axis_size("x"))]
    partner_queries = lax.ppermute(own_queries, "x", swap)
    odd = own_frame % 2
    even_count = lookup(list_counts, own_frame - odd)
    other_count = jnp.where(
        odd == 0, jnp.maximum(0, slots - even_count), jnp.maximum(0, even_count - slots)
    )
    mine_count = jnp.where(
        odd == 0, jnp.minimum(even_count, slots), pair_blocks - jnp.maximum(even_count, slots)
    )
    step = jnp.arange(slots, dtype=jnp.int32)
    visit = jnp.where(odd == 0, slots - 1 - step, step)
    own_visit = jnp.where(odd == 0, slots - 1 - jnp.minimum(step + other_count, slots - 1),
                          jnp.minimum(step + other_count, slots - 1))

    quarters = lax.axis_size("clip")
    quarter_rows = tokens_here // quarters
    halves = 2

    def half_rows(rows, half):
        rows = rows.reshape(quarters, halves, quarter_rows // halves, rows.shape[-1])
        return rows[:, half].reshape(tokens_here // halves, rows.shape[-1])

    finished = []
    for half in range(halves):
        mine_q = half_rows(own_queries, half)
        other_q = half_rows(partner_queries, half)
        other_out, other_max, other_sum = attend(
            other_q, arrived, visit, other_count.reshape(1)
        )
        got_max, got_sum, got_out = lax.ppermute(
            (other_max[:, ::HD], other_sum[:, ::HD], other_out), "x", swap
        )
        own_out, own_max, own_sum = attend(
            mine_q, arrived, own_visit, mine_count.reshape(1), own_keys, own_values
        )
        got_max = jnp.repeat(got_max, HD, axis=1)
        got_sum = jnp.repeat(got_sum, HD, axis=1)
        top = jnp.maximum(own_max, got_max)
        own_scale = jnp.exp(own_max - top)
        got_scale = jnp.exp(got_max - top)
        total_sum = own_sum * own_scale + got_sum * got_scale
        total_out = own_out * own_scale + got_out * got_scale
        attended = (total_out / total_sum).astype(jnp.bfloat16)
        partial_value = jnp.dot(attended, weight, preferred_element_type=jnp.float32)
        finished.append(
            lax.psum_scatter(
                partial_value.astype(jnp.bfloat16), "clip", scatter_dimension=0, tiled=True
            )
        )
    own_rows = jnp.concatenate(finished, axis=0)
    return own_rows[None]


def solution(mesh):
    frames = mesh.shape["fsdp"]
    fine = Mesh(
        np.asarray(mesh.devices).reshape(mesh.shape["clip"], frames // 16, 4, 4),
        ("clip",) + FRAME_AXES,
    )
    in_specs = (
        P(FRAME_AXES, None, "clip"),
        P(FRAME_AXES, None, "clip"),
        P(FRAME_AXES, None, "clip"),
        P(None, FRAME_AXES, "clip"),
        P(None, FRAME_AXES, "clip"),
        P(),
        P(),
        P(),
        P("clip", FRAME_AXES),
    )
    out_specs = P(FRAME_AXES, "clip", None)
    return jax.shard_map(local, mesh=fine, in_specs=in_specs, out_specs=out_specs, check_vma=False)
```

```python
import math

import jax
import jax.numpy as jnp
import numpy as np
from jax import lax
from jax.experimental import pallas as pl
from jax.experimental.pallas import tpu as pltpu
from jax.sharding import Mesh
from jax.sharding import PartitionSpec as P

HD = 128
CF = 8
NC = 16

FRAME_AXES = ("y", "zl", "x")

neg_fill = -1e30


def attend_kernel(order_ref, count_ref, q_ref, k_ref, v_ref, *rest, with_init, heads):
    if with_init:
        o0_ref, m0_ref, l0_ref, o_ref, m_ref, l_ref = rest
    else:
        o_ref, m_ref, l_ref = rest
    step = pl.program_id(0)

    @pl.when(step == 0)
    def _init():
        if with_init:
            m_ref[...] = m0_ref[...]
            l_ref[...] = l0_ref[...]
            o_ref[...] = o0_ref[...]
        else:
            m_ref[...] = jnp.full(m_ref.shape, neg_fill, jnp.float32)
            l_ref[...] = jnp.zeros(l_ref.shape, jnp.float32)
            o_ref[...] = jnp.zeros(o_ref.shape, jnp.float32)

    @pl.when(step < count_ref[0])
    def _slot():
        for head in range(heads):
            cols = pl.ds(head * HD, HD)
            scores = lax.dot_general(
                q_ref[:, cols], k_ref[0, 0, :, cols], (((1,), (1,)), ((), ())),
                preferred_element_type=jnp.float32,
            ) * (1.0 / math.sqrt(HD))
            running_max = m_ref[:, pl.ds(head * HD, 1)]
            new_max = jnp.maximum(running_max, jnp.max(scores, axis=1, keepdims=True))
            shrink = jnp.exp(running_max - new_max)
            weights = jnp.exp(scores - new_max)
            l_ref[:, cols] = l_ref[:, cols] * shrink + jnp.sum(weights, axis=1, keepdims=True)
            o_ref[:, cols] = o_ref[:, cols] * shrink + jnp.dot(
                weights.astype(jnp.bfloat16), v_ref[0, 0, :, cols],
                preferred_element_type=jnp.float32,
            )
            m_ref[:, cols] = jnp.broadcast_to(new_max, (new_max.shape[0], HD))


def attend(queries, arrived, order, count, init=None):
    tokens, width = queries.shape
    slots = arrived.shape[1]
    keys_each = arrived.shape[2]
    heads = width // HD
    with_init = init is not None

    def slot_at(s, order_ref, count_ref):
        return order_ref[jnp.clip(s, 0, jnp.maximum(count_ref[0] - 1, 0))]

    q_spec = pl.BlockSpec((tokens, width), lambda s, o, c: (0, 0))
    k_spec = pl.BlockSpec((1, 1, keys_each, width), lambda s, o, c: (0, slot_at(s, o, c), 0, 0))
    v_spec = pl.BlockSpec((1, 1, keys_each, width), lambda s, o, c: (1, slot_at(s, o, c), 0, 0))
    in_specs = [q_spec, k_spec, v_spec]
    operands = [queries, arrived, arrived]
    state_spec = pl.BlockSpec((tokens, width), lambda s, o, c: (0, 0))
    if with_init:
        in_specs += [state_spec] * 3
        operands += list(init)
    state_shape = jax.ShapeDtypeStruct((tokens, width), jnp.float32)
    return pl.pallas_call(
        lambda *refs: attend_kernel(*refs, with_init=with_init, heads=heads),
        grid_spec=pltpu.PrefetchScalarGridSpec(
            num_scalar_prefetch=2,
            grid=(slots,),
            in_specs=in_specs,
            out_specs=[state_spec] * 3,
        ),
        out_shape=[state_shape] * 3,
        compiler_params=pltpu.CompilerParams(dimension_semantics=("arbitrary",)),
        cost_estimate=pl.CostEstimate(
            flops=4 * slots * tokens * keys_each * width,
            transcendentals=slots * heads * tokens * keys_each,
            bytes_accessed=2 * slots * keys_each * width * 2 + 6 * tokens * width * 4,
        ),
    )(order, count, *operands)


def lookup(values_table, positions):
    table_width = values_table.shape[0]
    matches = positions[..., None] == jnp.arange(table_width, dtype=jnp.int32)
    return jnp.sum(jnp.where(matches, values_table, 0), axis=-1)


def pair_schedule(frames, slots, page_table, frame_lists, list_counts):
    max_slots = frame_lists.shape[1]
    dest = jnp.arange(frames, dtype=jnp.int32)[:, None]
    slot = jnp.arange(slots, dtype=jnp.int32)[None, :]
    even = dest - dest % 2
    combined = jnp.minimum((dest % 2) * slots + slot, max_slots)
    even_count = lookup(list_counts, even)
    for_even = combined < even_count
    listed_even = lookup(frame_lists.reshape(-1), even * max_slots + jnp.minimum(combined, max_slots - 1))
    listed_odd = lookup(
        frame_lists.reshape(-1),
        (even + 1) * max_slots + jnp.clip(combined - even_count, 0, max_slots - 1),
    )
    listed = jnp.where(for_even, listed_even, listed_odd)
    return lookup(page_table, (even // CF) * NC + listed)


def local(
    span_queries,
    span_keys,
    span_values,
    cache_keys,
    cache_values,
    page_table,
    frame_lists,
    list_counts,
    out_weight,
):
    frames = lax.axis_size(FRAME_AXES)
    own_frame = lax.axis_index(FRAME_AXES)
    tokens_here = span_queries.shape[1]
    row_width = span_queries.shape[2]
    heads_here = row_width // HD
    max_slots = frame_lists.shape[1]
    pair_blocks = max_slots + 1
    slots = (pair_blocks + 1) // 2
    own_queries = span_queries[0]
    own_keys = span_keys[0]
    own_values = span_values[0]

    weight = lax.all_gather(out_weight, ("zl", "x"), axis=1, tiled=True)

    blocks = pair_schedule(frames, slots, page_table, frame_lists, list_counts).T
    sent = jnp.stack([cache_keys[blocks], cache_values[blocks]], axis=0)
    arrived = lax.all_to_all(sent, FRAME_AXES, split_axis=2, concat_axis=2, tiled=True)
    arrived = arrived.reshape(2, slots, tokens_here, row_width)

    swap = [(i, i ^ 1) for i in range(lax.axis_size("x"))]
    partner_queries = lax.ppermute(own_queries, "x", swap)
    odd = own_frame % 2
    even_count = lookup(list_counts, own_frame - odd)
    other_count = jnp.where(
        odd == 0, jnp.maximum(0, slots - even_count), jnp.maximum(0, even_count - slots)
    )
    mine_count = jnp.where(
        odd == 0, jnp.minimum(even_count, slots), pair_blocks - jnp.maximum(even_count, slots)
    )
    step = jnp.arange(slots, dtype=jnp.int32)
    visit = jnp.where(odd == 0, slots - 1 - step, step)
    own_visit = jnp.where(odd == 0, slots - 1 - jnp.minimum(step + other_count, slots - 1),
                          jnp.minimum(step + other_count, slots - 1))

    own_span = jnp.stack([own_keys, own_values])[:, None]
    own_start = attend(
        own_queries, own_span, jnp.zeros((1,), jnp.int32), jnp.ones((1,), jnp.int32)
    )
    weight, own_start = lax.optimization_barrier((weight, own_start))
    weight = lax.all_gather(weight, "y", axis=1, tiled=True)
    other_out, other_max, other_sum = attend(
        partner_queries, arrived, visit, other_count.reshape(1)
    )
    got_max, got_sum, got_out = lax.ppermute(
        (other_max[:, ::HD], other_sum[:, ::HD], other_out), "x", swap
    )
    own_out, own_max, own_sum = attend(
        own_queries, arrived, own_visit, mine_count.reshape(1), own_start
    )
    got_max = jnp.repeat(got_max, HD, axis=1)
    got_sum = jnp.repeat(got_sum, HD, axis=1)
    top = jnp.maximum(own_max, got_max)
    own_scale = jnp.exp(own_max - top)
    got_scale = jnp.exp(got_max - top)
    total_sum = own_sum * own_scale + got_sum * got_scale
    total_out = own_out * own_scale + got_out * got_scale
    attended = (total_out / total_sum).astype(jnp.bfloat16)
    partial_value = jnp.dot(attended, weight, preferred_element_type=jnp.float32)
    own_rows = lax.psum_scatter(
        partial_value.astype(jnp.bfloat16), "clip", scatter_dimension=0, tiled=True
    )
    return own_rows[None]


def solution(mesh):
    frames = mesh.shape["fsdp"]
    fine = Mesh(
        np.asarray(mesh.devices).reshape(mesh.shape["clip"], frames // 16, 4, 4),
        ("clip",) + FRAME_AXES,
    )
    in_specs = (
        P(FRAME_AXES, None, "clip"),
        P(FRAME_AXES, None, "clip"),
        P(FRAME_AXES, None, "clip"),
        P(None, FRAME_AXES, "clip"),
        P(None, FRAME_AXES, "clip"),
        P(),
        P(),
        P(),
        P("clip", FRAME_AXES),
    )
    out_specs = P(FRAME_AXES, "clip", None)
    return jax.shard_map(local, mesh=fine, in_specs=in_specs, out_specs=out_specs, check_vma=False)
```

```python
import math

import jax
import jax.numpy as jnp
import numpy as np
from jax import lax
from jax.experimental import pallas as pl
from jax.experimental.pallas import tpu as pltpu
from jax.sharding import Mesh
from jax.sharding import PartitionSpec as P

HD = 128
CF = 8
NC = 16

FRAME_AXES = ("y", "zl", "x")

neg_fill = -1e30


def attend_kernel(order_ref, count_ref, q_ref, k_ref, v_ref, *rest, with_init, heads):
    if with_init:
        o0_ref, m0_ref, l0_ref, o_ref, m_ref, l_ref = rest
    else:
        o_ref, m_ref, l_ref = rest
    step = pl.program_id(0)

    @pl.when(step == 0)
    def _init():
        if with_init:
            m_ref[...] = m0_ref[...]
            l_ref[...] = l0_ref[...]
            o_ref[...] = o0_ref[...]
        else:
            m_ref[...] = jnp.full(m_ref.shape, neg_fill, jnp.float32)
            l_ref[...] = jnp.zeros(l_ref.shape, jnp.float32)
            o_ref[...] = jnp.zeros(o_ref.shape, jnp.float32)

    @pl.when(step < count_ref[0])
    def _slot():
        for head in range(heads):
            cols = pl.ds(head * HD, HD)
            scores = lax.dot_general(
                q_ref[:, cols], k_ref[0, 0, :, cols], (((1,), (1,)), ((), ())),
                preferred_element_type=jnp.float32,
            ) * (1.0 / math.sqrt(HD))
            running_max = m_ref[:, pl.ds(head * HD, 1)]
            new_max = jnp.maximum(running_max, jnp.max(scores, axis=1, keepdims=True))
            shrink = jnp.exp(running_max - new_max)
            weights = jnp.exp(scores - new_max)
            l_ref[:, cols] = l_ref[:, cols] * shrink + jnp.sum(weights, axis=1, keepdims=True)
            o_ref[:, cols] = o_ref[:, cols] * shrink + jnp.dot(
                weights.astype(jnp.bfloat16), v_ref[0, 0, :, cols],
                preferred_element_type=jnp.float32,
            )
            m_ref[:, cols] = jnp.broadcast_to(new_max, (new_max.shape[0], HD))


def attend(queries, arrived, order, count, init=None):
    tokens, width = queries.shape
    slots = arrived.shape[1]
    keys_each = arrived.shape[2]
    heads = width // HD
    with_init = init is not None

    def slot_at(s, order_ref, count_ref):
        return order_ref[jnp.clip(s, 0, jnp.maximum(count_ref[0] - 1, 0))]

    q_spec = pl.BlockSpec((tokens, width), lambda s, o, c: (0, 0))
    k_spec = pl.BlockSpec((1, 1, keys_each, width), lambda s, o, c: (0, slot_at(s, o, c), 0, 0))
    v_spec = pl.BlockSpec((1, 1, keys_each, width), lambda s, o, c: (1, slot_at(s, o, c), 0, 0))
    in_specs = [q_spec, k_spec, v_spec]
    operands = [queries, arrived, arrived]
    state_spec = pl.BlockSpec((tokens, width), lambda s, o, c: (0, 0))
    if with_init:
        in_specs += [state_spec] * 3
        operands += list(init)
    state_shape = jax.ShapeDtypeStruct((tokens, width), jnp.float32)
    return pl.pallas_call(
        lambda *refs: attend_kernel(*refs, with_init=with_init, heads=heads),
        grid_spec=pltpu.PrefetchScalarGridSpec(
            num_scalar_prefetch=2,
            grid=(slots,),
            in_specs=in_specs,
            out_specs=[state_spec] * 3,
        ),
        out_shape=[state_shape] * 3,
        compiler_params=pltpu.CompilerParams(dimension_semantics=("arbitrary",)),
        cost_estimate=pl.CostEstimate(
            flops=4 * slots * tokens * keys_each * width,
            transcendentals=slots * heads * tokens * keys_each,
            bytes_accessed=2 * slots * keys_each * width * 2 + 6 * tokens * width * 4,
        ),
    )(order, count, *operands)


def lookup(values_table, positions):
    table_width = values_table.shape[0]
    matches = positions[..., None] == jnp.arange(table_width, dtype=jnp.int32)
    return jnp.sum(jnp.where(matches, values_table, 0), axis=-1)


def pair_schedule(frames, slots, page_table, frame_lists, list_counts):
    max_slots = frame_lists.shape[1]
    dest = jnp.arange(frames, dtype=jnp.int32)[:, None]
    slot = jnp.arange(slots, dtype=jnp.int32)[None, :]
    even = dest - dest % 2
    combined = jnp.minimum((dest % 2) * slots + slot, max_slots)
    even_count = lookup(list_counts, even)
    for_even = combined < even_count
    listed_even = lookup(frame_lists.reshape(-1), even * max_slots + jnp.minimum(combined, max_slots - 1))
    listed_odd = lookup(
        frame_lists.reshape(-1),
        (even + 1) * max_slots + jnp.clip(combined - even_count, 0, max_slots - 1),
    )
    listed = jnp.where(for_even, listed_even, listed_odd)
    return lookup(page_table, (even // CF) * NC + listed)


def local(
    span_queries,
    span_keys,
    span_values,
    cache_keys,
    cache_values,
    page_table,
    frame_lists,
    list_counts,
    out_weight,
):
    frames = lax.axis_size(FRAME_AXES)
    own_frame = lax.axis_index(FRAME_AXES)
    tokens_here = span_queries.shape[1]
    row_width = span_queries.shape[2]
    heads_here = row_width // HD
    max_slots = frame_lists.shape[1]
    pair_blocks = max_slots + 1
    slots = (pair_blocks + 1) // 2
    own_queries = span_queries[0]
    own_keys = span_keys[0]
    own_values = span_values[0]

    weight = lax.all_gather(out_weight, ("zl", "x"), axis=1, tiled=True)

    blocks = pair_schedule(frames, slots, page_table, frame_lists, list_counts).T
    sent = jnp.stack([cache_keys[blocks], cache_values[blocks]], axis=0)
    arrived = lax.all_to_all(sent, FRAME_AXES, split_axis=2, concat_axis=2, tiled=True)
    arrived = arrived.reshape(2, slots, tokens_here, row_width)

    swap = [(i, i ^ 1) for i in range(lax.axis_size("x"))]
    partner_queries = lax.ppermute(own_queries, "x", swap)
    odd = own_frame % 2
    even_count = lookup(list_counts, own_frame - odd)
    other_count = jnp.where(
        odd == 0, jnp.maximum(0, slots - even_count), jnp.maximum(0, even_count - slots)
    )
    mine_count = jnp.where(
        odd == 0, jnp.minimum(even_count, slots), pair_blocks - jnp.maximum(even_count, slots)
    )
    step = jnp.arange(slots, dtype=jnp.int32)
    visit = jnp.where(odd == 0, slots - 1 - step, step)

    own_span = jnp.stack([own_keys, own_values])[:, None]
    own_start = attend(
        own_queries, own_span, jnp.zeros((1,), jnp.int32), jnp.ones((1,), jnp.int32)
    )
    weight, own_start = lax.optimization_barrier((weight, own_start))
    weight = lax.all_gather(weight, "y", axis=1, tiled=True)
    meet = jnp.abs(slots - even_count)
    before = jnp.clip(meet - other_count, 0, mine_count)
    after = mine_count - before

    def visits_from(first):
        at = jnp.minimum(step + first, slots - 1)
        return jnp.where(odd == 0, slots - 1 - at, at)

    other_state = attend(partner_queries, arrived, visit, other_count.reshape(1))
    own_state = attend(
        own_queries, arrived, visits_from(other_count), before.reshape(1), own_start
    )
    other_state, own_state = lax.optimization_barrier((other_state, own_state))
    other_out, other_max, other_sum = other_state
    got_max, got_sum, got_out = lax.ppermute(
        (other_max[:, ::HD], other_sum[:, ::HD], other_out), "x", swap
    )
    own_out, own_max, own_sum = attend(
        own_queries, arrived, visits_from(other_count + before), after.reshape(1), own_state
    )
    got_max = jnp.repeat(got_max, HD, axis=1)
    got_sum = jnp.repeat(got_sum, HD, axis=1)
    top = jnp.maximum(own_max, got_max)
    own_scale = jnp.exp(own_max - top)
    got_scale = jnp.exp(got_max - top)
    total_sum = own_sum * own_scale + got_sum * got_scale
    total_out = own_out * own_scale + got_out * got_scale
    attended = (total_out / total_sum).astype(jnp.bfloat16)
    partial_value = jnp.dot(attended, weight, preferred_element_type=jnp.float32)
    own_rows = lax.psum_scatter(
        partial_value.astype(jnp.bfloat16), "clip", scatter_dimension=0, tiled=True
    )
    return own_rows[None]


def solution(mesh):
    frames = mesh.shape["fsdp"]
    fine = Mesh(
        np.asarray(mesh.devices).reshape(mesh.shape["clip"], frames // 16, 4, 4),
        ("clip",) + FRAME_AXES,
    )
    in_specs = (
        P(FRAME_AXES, None, "clip"),
        P(FRAME_AXES, None, "clip"),
        P(FRAME_AXES, None, "clip"),
        P(None, FRAME_AXES, "clip"),
        P(None, FRAME_AXES, "clip"),
        P(),
        P(),
        P(),
        P("clip", FRAME_AXES),
    )
    out_specs = P(FRAME_AXES, "clip", None)
    return jax.shard_map(local, mesh=fine, in_specs=in_specs, out_specs=out_specs, check_vma=False)
```

```python
import math

import jax
import jax.numpy as jnp
import numpy as np
from jax import lax
from jax.experimental import pallas as pl
from jax.experimental.pallas import tpu as pltpu
from jax.sharding import Mesh
from jax.sharding import PartitionSpec as P

HD = 128
CF = 8
NC = 16

FRAME_AXES = ("y", "zl", "x")
CLIP_AXES = ("zh", "core")

neg_fill = -1e30


def attend_kernel(order_ref, count_ref, q_ref, k_ref, v_ref, *rest, with_init, heads):
    if with_init:
        o0_ref, m0_ref, l0_ref, o_ref, m_ref, l_ref = rest
    else:
        o_ref, m_ref, l_ref = rest
    step = pl.program_id(0)

    @pl.when(step == 0)
    def _init():
        if with_init:
            m_ref[...] = m0_ref[...]
            l_ref[...] = l0_ref[...]
            o_ref[...] = o0_ref[...]
        else:
            m_ref[...] = jnp.full(m_ref.shape, neg_fill, jnp.float32)
            l_ref[...] = jnp.zeros(l_ref.shape, jnp.float32)
            o_ref[...] = jnp.zeros(o_ref.shape, jnp.float32)

    @pl.when(step < count_ref[0])
    def _slot():
        for head in range(heads):
            cols = pl.ds(head * HD, HD)
            scores = lax.dot_general(
                q_ref[:, cols], k_ref[0, 0, :, cols], (((1,), (1,)), ((), ())),
                preferred_element_type=jnp.float32,
            ) * (1.0 / math.sqrt(HD))
            running_max = m_ref[:, pl.ds(head * HD, 1)]
            new_max = jnp.maximum(running_max, jnp.max(scores, axis=1, keepdims=True))
            shrink = jnp.exp(running_max - new_max)
            weights = jnp.exp(scores - new_max)
            l_ref[:, cols] = l_ref[:, cols] * shrink + jnp.sum(weights, axis=1, keepdims=True)
            o_ref[:, cols] = o_ref[:, cols] * shrink + jnp.dot(
                weights.astype(jnp.bfloat16), v_ref[0, 0, :, cols],
                preferred_element_type=jnp.float32,
            )
            m_ref[:, cols] = jnp.broadcast_to(new_max, (new_max.shape[0], HD))


def attend(queries, arrived, order, count, init=None):
    tokens, width = queries.shape
    slots = arrived.shape[1]
    keys_each = arrived.shape[2]
    heads = width // HD
    with_init = init is not None

    def slot_at(s, order_ref, count_ref):
        return order_ref[jnp.clip(s, 0, jnp.maximum(count_ref[0] - 1, 0))]

    q_spec = pl.BlockSpec((tokens, width), lambda s, o, c: (0, 0))
    k_spec = pl.BlockSpec((1, 1, keys_each, width), lambda s, o, c: (0, slot_at(s, o, c), 0, 0))
    v_spec = pl.BlockSpec((1, 1, keys_each, width), lambda s, o, c: (1, slot_at(s, o, c), 0, 0))
    in_specs = [q_spec, k_spec, v_spec]
    operands = [queries, arrived, arrived]
    state_spec = pl.BlockSpec((tokens, width), lambda s, o, c: (0, 0))
    if with_init:
        in_specs += [state_spec] * 3
        operands += list(init)
    state_shape = jax.ShapeDtypeStruct((tokens, width), jnp.float32)
    return pl.pallas_call(
        lambda *refs: attend_kernel(*refs, with_init=with_init, heads=heads),
        grid_spec=pltpu.PrefetchScalarGridSpec(
            num_scalar_prefetch=2,
            grid=(slots,),
            in_specs=in_specs,
            out_specs=[state_spec] * 3,
        ),
        out_shape=[state_shape] * 3,
        compiler_params=pltpu.CompilerParams(dimension_semantics=("arbitrary",)),
        cost_estimate=pl.CostEstimate(
            flops=4 * slots * tokens * keys_each * width,
            transcendentals=slots * heads * tokens * keys_each,
            bytes_accessed=2 * slots * keys_each * width * 2 + 6 * tokens * width * 4,
        ),
    )(order, count, *operands)


def lookup(values_table, positions):
    table_width = values_table.shape[0]
    matches = positions[..., None] == jnp.arange(table_width, dtype=jnp.int32)
    return jnp.sum(jnp.where(matches, values_table, 0), axis=-1)


def pair_schedule(frames, slots, page_table, frame_lists, list_counts):
    max_slots = frame_lists.shape[1]
    dest = jnp.arange(frames, dtype=jnp.int32)[:, None]
    slot = jnp.arange(slots, dtype=jnp.int32)[None, :]
    even = dest - dest % 2
    combined = jnp.minimum((dest % 2) * slots + slot, max_slots)
    even_count = lookup(list_counts, even)
    for_even = combined < even_count
    listed_even = lookup(frame_lists.reshape(-1), even * max_slots + jnp.minimum(combined, max_slots - 1))
    listed_odd = lookup(
        frame_lists.reshape(-1),
        (even + 1) * max_slots + jnp.clip(combined - even_count, 0, max_slots - 1),
    )
    listed = jnp.where(for_even, listed_even, listed_odd)
    return lookup(page_table, (even // CF) * NC + listed)


def local(
    span_queries,
    span_keys,
    span_values,
    cache_keys,
    cache_values,
    page_table,
    frame_lists,
    list_counts,
    out_weight,
):
    frames = lax.axis_size(FRAME_AXES)
    own_frame = lax.axis_index(FRAME_AXES)
    tokens_here = span_queries.shape[1]
    row_width = span_queries.shape[2]
    heads_here = row_width // HD
    max_slots = frame_lists.shape[1]
    pair_blocks = max_slots + 1
    slots = (pair_blocks + 1) // 2
    own_queries = span_queries[0]
    own_keys = span_keys[0]
    own_values = span_values[0]

    weight = lax.all_gather(out_weight, ("zl", "x"), axis=1, tiled=True)

    blocks = pair_schedule(frames, slots, page_table, frame_lists, list_counts).T
    sent = jnp.stack([cache_keys[blocks], cache_values[blocks]], axis=0)
    arrived = lax.all_to_all(sent, FRAME_AXES, split_axis=2, concat_axis=2, tiled=True)
    arrived = arrived.reshape(2, slots, tokens_here, row_width)

    swap = [(i, i ^ 1) for i in range(lax.axis_size("x"))]
    partner_queries = lax.ppermute(own_queries, "x", swap)
    odd = own_frame % 2
    even_count = lookup(list_counts, own_frame - odd)
    other_count = jnp.where(
        odd == 0, jnp.maximum(0, slots - even_count), jnp.maximum(0, even_count - slots)
    )
    mine_count = jnp.where(
        odd == 0, jnp.minimum(even_count, slots), pair_blocks - jnp.maximum(even_count, slots)
    )
    step = jnp.arange(slots, dtype=jnp.int32)
    visit = jnp.where(odd == 0, slots - 1 - step, step)

    own_span = jnp.stack([own_keys, own_values])[:, None]
    own_start = attend(
        own_queries, own_span, jnp.zeros((1,), jnp.int32), jnp.ones((1,), jnp.int32)
    )
    weight, own_start = lax.optimization_barrier((weight, own_start))
    weight = lax.all_gather(weight, "y", axis=1, tiled=True)
    meet = jnp.abs(slots - even_count)
    before = jnp.clip(meet - other_count, 0, mine_count)
    after = mine_count - before

    def visits_from(first):
        at = jnp.minimum(step + first, slots - 1)
        return jnp.where(odd == 0, slots - 1 - at, at)

    other_state = attend(partner_queries, arrived, visit, other_count.reshape(1))
    own_state = attend(
        own_queries, arrived, visits_from(other_count), before.reshape(1), own_start
    )
    other_state, own_state = lax.optimization_barrier((other_state, own_state))
    other_out, other_max, other_sum = other_state
    got_max, got_sum, got_out = lax.ppermute(
        (other_max[:, ::HD], other_sum[:, ::HD], other_out), "x", swap
    )
    own_out, own_max, own_sum = attend(
        own_queries, arrived, visits_from(other_count + before), after.reshape(1), own_state
    )
    got_max = jnp.repeat(got_max, HD, axis=1)
    got_sum = jnp.repeat(got_sum, HD, axis=1)
    top = jnp.maximum(own_max, got_max)
    own_scale = jnp.exp(own_max - top)
    got_scale = jnp.exp(got_max - top)
    total_sum = own_sum * own_scale + got_sum * got_scale
    total_out = own_out * own_scale + got_out * got_scale
    attended = (total_out / total_sum).astype(jnp.bfloat16)
    quarters = lax.axis_size("zh") * lax.axis_size("core")
    quarter_rows = tokens_here // quarters
    attended = attended.reshape(lax.axis_size("zh"), lax.axis_size("core"), quarter_rows, row_width)
    attended = attended.transpose(1, 0, 2, 3).reshape(tokens_here, row_width)
    partial_value = jnp.dot(attended, weight, preferred_element_type=jnp.float32)
    on_chip = lax.psum_scatter(
        partial_value.astype(jnp.bfloat16), "core", scatter_dimension=0, tiled=True
    )
    on_chip = on_chip.reshape(lax.axis_size("zh"), quarter_rows, -1)
    chip_half = lax.axis_index("zh")
    mine = lax.dynamic_index_in_dim(on_chip, chip_half, 0, keepdims=False)
    theirs = lax.dynamic_index_in_dim(on_chip, 1 - chip_half, 0, keepdims=False)
    ring = lax.axis_size("zh") * lax.axis_size("zl")
    z_axes = ("zh", "zl")

    def shifted(rows, by):
        return lax.ppermute(rows, z_axes, [(i, (i + by) % ring) for i in range(ring)])

    half = quarter_rows // 2
    up = shifted(shifted(theirs[:half], 1), ring // 2 - 1)
    down = shifted(shifted(theirs[half:], -1), 1 - ring // 2)
    received = jnp.concatenate([up, down], axis=0)
    own_rows = (mine.astype(jnp.float32) + received.astype(jnp.float32)).astype(jnp.bfloat16)
    return own_rows[None]


def solution(mesh):
    frames = mesh.shape["fsdp"]
    fine = Mesh(
        np.asarray(mesh.devices).reshape(2, mesh.shape["clip"] // 2, frames // 16, 4, 4),
        CLIP_AXES + FRAME_AXES,
    )
    in_specs = (
        P(FRAME_AXES, None, CLIP_AXES),
        P(FRAME_AXES, None, CLIP_AXES),
        P(FRAME_AXES, None, CLIP_AXES),
        P(None, FRAME_AXES, CLIP_AXES),
        P(None, FRAME_AXES, CLIP_AXES),
        P(),
        P(),
        P(),
        P(CLIP_AXES, FRAME_AXES),
    )
    out_specs = P(FRAME_AXES, CLIP_AXES, None)
    return jax.shard_map(local, mesh=fine, in_specs=in_specs, out_specs=out_specs, check_vma=False)
```

```python
import math

import jax
import jax.numpy as jnp
import numpy as np
from jax import lax
from jax.experimental import pallas as pl
from jax.experimental.pallas import tpu as pltpu
from jax.sharding import Mesh
from jax.sharding import PartitionSpec as P

HD = 128
CF = 8
NC = 16

FRAME_AXES = ("y", "zl", "x")
CLIP_AXES = ("zh", "core")

neg_fill = -1e30


def attend_kernel(order_ref, count_ref, q_ref, k_ref, v_ref, *rest, with_init, heads):
    if with_init:
        o0_ref, m0_ref, l0_ref, o_ref, m_ref, l_ref = rest
    else:
        o_ref, m_ref, l_ref = rest
    step = pl.program_id(0)

    @pl.when(step == 0)
    def _init():
        if with_init:
            m_ref[...] = m0_ref[...]
            l_ref[...] = l0_ref[...]
            o_ref[...] = o0_ref[...]
        else:
            m_ref[...] = jnp.full(m_ref.shape, neg_fill, jnp.float32)
            l_ref[...] = jnp.zeros(l_ref.shape, jnp.float32)
            o_ref[...] = jnp.zeros(o_ref.shape, jnp.float32)

    @pl.when(step < count_ref[0])
    def _slot():
        def one_head(head, carry):
            cols = pl.ds(pl.multiple_of(head * HD, HD), HD)
            scores = lax.dot_general(
                q_ref[:, cols], k_ref[0, 0, :, cols], (((1,), (1,)), ((), ())),
                preferred_element_type=jnp.float32,
            ) * (1.0 / math.sqrt(HD))
            running_max = m_ref[:, cols][:, :1]
            new_max = jnp.maximum(running_max, jnp.max(scores, axis=1, keepdims=True))
            shrink = jnp.exp(running_max - new_max)
            weights = jnp.exp(scores - new_max)
            l_ref[:, cols] = l_ref[:, cols] * shrink + jnp.sum(weights, axis=1, keepdims=True)
            o_ref[:, cols] = o_ref[:, cols] * shrink + jnp.dot(
                weights.astype(jnp.bfloat16), v_ref[0, 0, :, cols],
                preferred_element_type=jnp.float32,
            )
            m_ref[:, cols] = jnp.broadcast_to(new_max, (new_max.shape[0], HD))
            return carry

        lax.fori_loop(0, heads, one_head, 0)


def attend(queries, arrived, order, count, init=None):
    tokens, width = queries.shape
    slots = arrived.shape[1]
    keys_each = arrived.shape[2]
    heads = width // HD
    with_init = init is not None

    def slot_at(s, order_ref, count_ref):
        return order_ref[jnp.clip(s, 0, jnp.maximum(count_ref[0] - 1, 0))]

    q_spec = pl.BlockSpec((tokens, width), lambda s, o, c: (0, 0))
    k_spec = pl.BlockSpec((1, 1, keys_each, width), lambda s, o, c: (0, slot_at(s, o, c), 0, 0))
    v_spec = pl.BlockSpec((1, 1, keys_each, width), lambda s, o, c: (1, slot_at(s, o, c), 0, 0))
    in_specs = [q_spec, k_spec, v_spec]
    operands = [queries, arrived, arrived]
    state_spec = pl.BlockSpec((tokens, width), lambda s, o, c: (0, 0))
    if with_init:
        in_specs += [state_spec] * 3
        operands += list(init)
    state_shape = jax.ShapeDtypeStruct((tokens, width), jnp.float32)
    return pl.pallas_call(
        lambda *refs: attend_kernel(*refs, with_init=with_init, heads=heads),
        grid_spec=pltpu.PrefetchScalarGridSpec(
            num_scalar_prefetch=2,
            grid=(slots,),
            in_specs=in_specs,
            out_specs=[state_spec] * 3,
        ),
        out_shape=[state_shape] * 3,
        compiler_params=pltpu.CompilerParams(dimension_semantics=("arbitrary",)),
        cost_estimate=pl.CostEstimate(
            flops=4 * slots * tokens * keys_each * width,
            transcendentals=slots * heads * tokens * keys_each,
            bytes_accessed=2 * slots * keys_each * width * 2 + 6 * tokens * width * 4,
        ),
    )(order, count, *operands)


def lookup(values_table, positions):
    table_width = values_table.shape[0]
    matches = positions[..., None] == jnp.arange(table_width, dtype=jnp.int32)
    return jnp.sum(jnp.where(matches, values_table, 0), axis=-1)


def pair_schedule(frames, slots, page_table, frame_lists, list_counts):
    max_slots = frame_lists.shape[1]
    dest = jnp.arange(frames, dtype=jnp.int32)[:, None]
    slot = jnp.arange(slots, dtype=jnp.int32)[None, :]
    even = dest - dest % 2
    combined = jnp.minimum((dest % 2) * slots + slot, max_slots)
    even_count = lookup(list_counts, even)
    for_even = combined < even_count
    listed_even = lookup(frame_lists.reshape(-1), even * max_slots + jnp.minimum(combined, max_slots - 1))
    listed_odd = lookup(
        frame_lists.reshape(-1),
        (even + 1) * max_slots + jnp.clip(combined - even_count, 0, max_slots - 1),
    )
    listed = jnp.where(for_even, listed_even, listed_odd)
    return lookup(page_table, (even // CF) * NC + listed)


def local(
    span_queries,
    span_keys,
    span_values,
    cache_keys,
    cache_values,
    page_table,
    frame_lists,
    list_counts,
    out_weight,
):
    frames = lax.axis_size(FRAME_AXES)
    own_frame = lax.axis_index(FRAME_AXES)
    tokens_here = span_queries.shape[1]
    row_width = span_queries.shape[2]
    heads_here = row_width // HD
    max_slots = frame_lists.shape[1]
    pair_blocks = max_slots + 1
    slots = (pair_blocks + 1) // 2
    own_queries = span_queries[0]
    own_keys = span_keys[0]
    own_values = span_values[0]

    weight = lax.all_gather(out_weight, ("zl", "x"), axis=1, tiled=True)

    blocks = pair_schedule(frames, slots, page_table, frame_lists, list_counts).T
    sent = jnp.stack([cache_keys[blocks], cache_values[blocks]], axis=0)
    arrived = lax.all_to_all(sent, FRAME_AXES, split_axis=2, concat_axis=2, tiled=True)
    arrived = arrived.reshape(2, slots, tokens_here, row_width)

    swap = [(i, i ^ 1) for i in range(lax.axis_size("x"))]
    partner_queries = lax.ppermute(own_queries, "x", swap)
    odd = own_frame % 2
    even_count = lookup(list_counts, own_frame - odd)
    other_count = jnp.where(
        odd == 0, jnp.maximum(0, slots - even_count), jnp.maximum(0, even_count - slots)
    )
    mine_count = jnp.where(
        odd == 0, jnp.minimum(even_count, slots), pair_blocks - jnp.maximum(even_count, slots)
    )
    step = jnp.arange(slots, dtype=jnp.int32)
    visit = jnp.where(odd == 0, slots - 1 - step, step)

    own_span = jnp.stack([own_keys, own_values])[:, None]
    own_start = attend(
        own_queries, own_span, jnp.zeros((1,), jnp.int32), jnp.ones((1,), jnp.int32)
    )
    weight, own_start = lax.optimization_barrier((weight, own_start))
    weight = lax.all_gather(weight, "y", axis=1, tiled=True)
    meet = jnp.abs(slots - even_count)
    before = jnp.clip(meet - other_count, 0, mine_count)
    after = mine_count - before

    def visits_from(first):
        at = jnp.minimum(step + first, slots - 1)
        return jnp.where(odd == 0, slots - 1 - at, at)

    other_state = attend(partner_queries, arrived, visit, other_count.reshape(1))
    own_state = attend(
        own_queries, arrived, visits_from(other_count), before.reshape(1), own_start
    )
    other_state, own_state = lax.optimization_barrier((other_state, own_state))
    other_out, other_max, other_sum = other_state
    got_max, got_sum, got_out = lax.ppermute(
        (other_max[:, ::HD], other_sum[:, ::HD], other_out), "x", swap
    )
    own_out, own_max, own_sum = attend(
        own_queries, arrived, visits_from(other_count + before), after.reshape(1), own_state
    )
    got_max = jnp.repeat(got_max, HD, axis=1)
    got_sum = jnp.repeat(got_sum, HD, axis=1)
    top = jnp.maximum(own_max, got_max)
    own_scale = jnp.exp(own_max - top)
    got_scale = jnp.exp(got_max - top)
    total_sum = own_sum * own_scale + got_sum * got_scale
    total_out = own_out * own_scale + got_out * got_scale
    attended = (total_out / total_sum).astype(jnp.bfloat16)
    quarters = lax.axis_size("zh") * lax.axis_size("core")
    quarter_rows = tokens_here // quarters
    attended = attended.reshape(lax.axis_size("zh"), lax.axis_size("core"), quarter_rows, row_width)
    attended = attended.transpose(1, 0, 2, 3).reshape(tokens_here, row_width)
    partial_value = jnp.dot(attended, weight, preferred_element_type=jnp.float32)
    on_chip = lax.psum_scatter(
        partial_value.astype(jnp.bfloat16), "core", scatter_dimension=0, tiled=True
    )
    on_chip = on_chip.reshape(lax.axis_size("zh"), quarter_rows, -1)
    chip_half = lax.axis_index("zh")
    mine = lax.dynamic_index_in_dim(on_chip, chip_half, 0, keepdims=False)
    theirs = lax.dynamic_index_in_dim(on_chip, 1 - chip_half, 0, keepdims=False)
    ring = lax.axis_size("zh") * lax.axis_size("zl")
    z_axes = ("zh", "zl")

    def shifted(rows, by):
        return lax.ppermute(rows, z_axes, [(i, (i + by) % ring) for i in range(ring)])

    half = quarter_rows // 2
    up = shifted(shifted(theirs[:half], 1), ring // 2 - 1)
    down = shifted(shifted(theirs[half:], -1), 1 - ring // 2)
    received = jnp.concatenate([up, down], axis=0)
    own_rows = (mine.astype(jnp.float32) + received.astype(jnp.float32)).astype(jnp.bfloat16)
    return own_rows[None]


def solution(mesh):
    frames = mesh.shape["fsdp"]
    fine = Mesh(
        np.asarray(mesh.devices).reshape(2, mesh.shape["clip"] // 2, frames // 16, 4, 4),
        CLIP_AXES + FRAME_AXES,
    )
    in_specs = (
        P(FRAME_AXES, None, CLIP_AXES),
        P(FRAME_AXES, None, CLIP_AXES),
        P(FRAME_AXES, None, CLIP_AXES),
        P(None, FRAME_AXES, CLIP_AXES),
        P(None, FRAME_AXES, CLIP_AXES),
        P(),
        P(),
        P(),
        P(CLIP_AXES, FRAME_AXES),
    )
    out_specs = P(FRAME_AXES, CLIP_AXES, None)
    return jax.shard_map(local, mesh=fine, in_specs=in_specs, out_specs=out_specs, check_vma=False)
```

```python
import math

import jax
import jax.numpy as jnp
import numpy as np
from jax import lax
from jax.experimental import pallas as pl
from jax.experimental.pallas import tpu as pltpu
from jax.sharding import Mesh
from jax.sharding import PartitionSpec as P

HD = 128
CF = 8
NC = 16

FRAME_AXES = ("y", "zl", "x")
CLIP_AXES = ("zh", "core")

neg_fill = -1e30


def attend_kernel(order_ref, count_ref, q_ref, k_ref, v_ref, *rest, with_init, heads):
    if with_init:
        o0_ref, m0_ref, l0_ref, o_ref, m_ref, l_ref = rest
    else:
        o_ref, m_ref, l_ref = rest
    step = pl.program_id(0)

    @pl.when(step == 0)
    def _init():
        if with_init:
            m_ref[...] = m0_ref[...]
            l_ref[...] = l0_ref[...]
            o_ref[...] = o0_ref[...]
        else:
            m_ref[...] = jnp.full(m_ref.shape, neg_fill, jnp.float32)
            l_ref[...] = jnp.zeros(l_ref.shape, jnp.float32)
            o_ref[...] = jnp.zeros(o_ref.shape, jnp.float32)

    @pl.when(step < count_ref[0])
    def _slot():
        for head in range(heads):
            cols = pl.ds(head * HD, HD)
            scores = lax.dot_general(
                q_ref[:, cols], k_ref[0, 0, :, cols], (((1,), (1,)), ((), ())),
                preferred_element_type=jnp.float32,
            ) * (1.0 / math.sqrt(HD))
            running_max = m_ref[:, pl.ds(head * HD, 1)]
            new_max = jnp.maximum(running_max, jnp.max(scores, axis=1, keepdims=True))
            shrink = jnp.exp(running_max - new_max)
            weights = jnp.exp(scores - new_max)
            l_ref[:, cols] = l_ref[:, cols] * shrink + jnp.sum(weights, axis=1, keepdims=True)
            o_ref[:, cols] = o_ref[:, cols] * shrink + jnp.dot(
                weights.astype(jnp.bfloat16), v_ref[0, 0, :, cols],
                preferred_element_type=jnp.float32,
            )
            m_ref[:, cols] = jnp.broadcast_to(new_max, (new_max.shape[0], HD))


def attend(queries, arrived, order, count, init=None):
    tokens, width = queries.shape
    slots = arrived.shape[1]
    keys_each = arrived.shape[2]
    heads = width // HD
    with_init = init is not None

    def slot_at(s, order_ref, count_ref):
        return order_ref[jnp.clip(s, 0, jnp.maximum(count_ref[0] - 1, 0))]

    q_spec = pl.BlockSpec((tokens, width), lambda s, o, c: (0, 0))
    k_spec = pl.BlockSpec((1, 1, keys_each, width), lambda s, o, c: (0, slot_at(s, o, c), 0, 0))
    v_spec = pl.BlockSpec((1, 1, keys_each, width), lambda s, o, c: (1, slot_at(s, o, c), 0, 0))
    in_specs = [q_spec, k_spec, v_spec]
    operands = [queries, arrived, arrived]
    state_spec = pl.BlockSpec((tokens, width), lambda s, o, c: (0, 0))
    if with_init:
        in_specs += [state_spec] * 3
        operands += list(init)
    state_shape = jax.ShapeDtypeStruct((tokens, width), jnp.float32)
    return pl.pallas_call(
        lambda *refs: attend_kernel(*refs, with_init=with_init, heads=heads),
        grid_spec=pltpu.PrefetchScalarGridSpec(
            num_scalar_prefetch=2,
            grid=(slots,),
            in_specs=in_specs,
            out_specs=[state_spec] * 3,
        ),
        out_shape=[state_shape] * 3,
        compiler_params=pltpu.CompilerParams(dimension_semantics=("arbitrary",)),
        cost_estimate=pl.CostEstimate(
            flops=4 * slots * tokens * keys_each * width,
            transcendentals=slots * heads * tokens * keys_each,
            bytes_accessed=2 * slots * keys_each * width * 2 + 6 * tokens * width * 4,
        ),
    )(order, count, *operands)


def lookup(values_table, positions):
    table_width = values_table.shape[0]
    matches = positions[..., None] == jnp.arange(table_width, dtype=jnp.int32)
    return jnp.sum(jnp.where(matches, values_table, 0), axis=-1)


def pair_schedule(frames, slots, page_table, frame_lists, list_counts):
    max_slots = frame_lists.shape[1]
    dest = jnp.arange(frames, dtype=jnp.int32)[:, None]
    slot = jnp.arange(slots, dtype=jnp.int32)[None, :]
    even = dest - dest % 2
    combined = jnp.minimum((dest % 2) * slots + slot, max_slots)
    even_count = lookup(list_counts, even)
    for_even = combined < even_count
    listed_even = lookup(frame_lists.reshape(-1), even * max_slots + jnp.minimum(combined, max_slots - 1))
    listed_odd = lookup(
        frame_lists.reshape(-1),
        (even + 1) * max_slots + jnp.clip(combined - even_count, 0, max_slots - 1),
    )
    listed = jnp.where(for_even, listed_even, listed_odd)
    return lookup(page_table, (even // CF) * NC + listed)


def local(
    span_queries,
    span_keys,
    span_values,
    cache_keys,
    cache_values,
    page_table,
    frame_lists,
    list_counts,
    out_weight,
):
    frames = lax.axis_size(FRAME_AXES)
    own_frame = lax.axis_index(FRAME_AXES)
    tokens_here = span_queries.shape[1]
    row_width = span_queries.shape[2]
    heads_here = row_width // HD
    max_slots = frame_lists.shape[1]
    pair_blocks = max_slots + 1
    slots = (pair_blocks + 1) // 2
    own_queries = span_queries[0]
    own_keys = span_keys[0]
    own_values = span_values[0]

    weight = lax.all_gather(out_weight, ("zl", "x"), axis=1, tiled=True)

    blocks = pair_schedule(frames, slots, page_table, frame_lists, list_counts).T
    sent = jnp.stack([cache_keys[blocks], cache_values[blocks]], axis=0)
    arrived = lax.all_to_all(sent, FRAME_AXES, split_axis=2, concat_axis=2, tiled=True)
    arrived = arrived.reshape(2, slots, tokens_here, row_width)

    swap = [(i, i ^ 1) for i in range(lax.axis_size("x"))]
    partner_queries = lax.ppermute(own_queries, "x", swap)
    odd = own_frame % 2
    even_count = lookup(list_counts, own_frame - odd)
    other_count = jnp.where(
        odd == 0, jnp.maximum(0, slots - even_count), jnp.maximum(0, even_count - slots)
    )
    mine_count = jnp.where(
        odd == 0, jnp.minimum(even_count, slots), pair_blocks - jnp.maximum(even_count, slots)
    )
    step = jnp.arange(slots, dtype=jnp.int32)
    visit = jnp.where(odd == 0, slots - 1 - step, step)

    own_span = jnp.stack([own_keys, own_values])[:, None]
    own_start = attend(
        own_queries, own_span, jnp.zeros((1,), jnp.int32), jnp.ones((1,), jnp.int32)
    )
    weight, own_start = lax.optimization_barrier((weight, own_start))
    weight = lax.all_gather(weight, "y", axis=1, tiled=True)
    meet = jnp.abs(slots - even_count)
    before = jnp.clip(meet - other_count, 0, mine_count)
    after = mine_count - before

    def visits_from(first):
        at = jnp.minimum(step + first, slots - 1)
        return jnp.where(odd == 0, slots - 1 - at, at)

    other_state = attend(partner_queries, arrived, visit, other_count.reshape(1))
    own_state = attend(
        own_queries, arrived, visits_from(other_count), before.reshape(1), own_start
    )
    other_state, own_state = lax.optimization_barrier((other_state, own_state))
    other_out, other_max, other_sum = other_state
    got_max, got_sum, got_out = lax.ppermute(
        (other_max[:, ::HD], other_sum[:, ::HD], other_out), "x", swap
    )
    own_out, own_max, own_sum = attend(
        own_queries, arrived, visits_from(other_count + before), after.reshape(1), own_state
    )
    got_max = jnp.repeat(got_max, HD, axis=1)
    got_sum = jnp.repeat(got_sum, HD, axis=1)
    top = jnp.maximum(own_max, got_max)
    own_scale = jnp.exp(own_max - top)
    got_scale = jnp.exp(got_max - top)
    total_sum = own_sum * own_scale + got_sum * got_scale
    total_out = own_out * own_scale + got_out * got_scale
    attended = (total_out / total_sum).astype(jnp.bfloat16)
    partial_value = jnp.dot(attended, weight, preferred_element_type=jnp.float32)
    partial_value = partial_value.astype(jnp.bfloat16)
    quarters = lax.axis_size("zh") * lax.axis_size("core")
    quarter_rows = tokens_here // quarters
    chip_half = lax.axis_index("zh")
    core = lax.axis_index("core")
    cores = lax.axis_size("core")
    core_swap = [(i, cores - 1 - i) for i in range(cores)]

    def quarter(zh, k):
        return lax.dynamic_slice_in_dim(partial_value, (zh * cores + k) * quarter_rows, quarter_rows)

    theirs = quarter(1 - chip_half, core).astype(jnp.float32) + lax.ppermute(
        quarter(1 - chip_half, cores - 1 - core), "core", core_swap
    ).astype(jnp.float32)
    theirs = theirs.astype(jnp.bfloat16)
    ring = lax.axis_size("zh") * lax.axis_size("zl")
    z_axes = ("zh", "zl")

    def shifted(rows, by):
        return lax.ppermute(rows, z_axes, [(i, (i + by) % ring) for i in range(ring)])

    pieces = 4
    piece_rows = quarter_rows // pieces
    received = []
    for piece in range(pieces):
        rows = theirs[piece * piece_rows:(piece + 1) * piece_rows]
        first = 1 if piece < pieces // 2 else -1
        received.append(shifted(shifted(rows, first), first * (ring // 2 - 1)))
    received = jnp.concatenate(received, axis=0)
    mine = quarter(chip_half, core).astype(jnp.float32) + lax.ppermute(
        quarter(chip_half, cores - 1 - core), "core", core_swap
    ).astype(jnp.float32)
    own_rows = (mine + received.astype(jnp.float32)).astype(jnp.bfloat16)
    return own_rows[None]


def solution(mesh):
    frames = mesh.shape["fsdp"]
    fine = Mesh(
        np.asarray(mesh.devices).reshape(2, mesh.shape["clip"] // 2, frames // 16, 4, 4),
        CLIP_AXES + FRAME_AXES,
    )
    in_specs = (
        P(FRAME_AXES, None, CLIP_AXES),
        P(FRAME_AXES, None, CLIP_AXES),
        P(FRAME_AXES, None, CLIP_AXES),
        P(None, FRAME_AXES, CLIP_AXES),
        P(None, FRAME_AXES, CLIP_AXES),
        P(),
        P(),
        P(),
        P(CLIP_AXES, FRAME_AXES),
    )
    out_specs = P(FRAME_AXES, CLIP_AXES, None)
    return jax.shard_map(local, mesh=fine, in_specs=in_specs, out_specs=out_specs, check_vma=False)
```

```python
import math

import jax
import jax.numpy as jnp
import numpy as np
from jax import lax
from jax.experimental import pallas as pl
from jax.experimental.pallas import tpu as pltpu
from jax.sharding import Mesh
from jax.sharding import PartitionSpec as P

HD = 128
CF = 8
NC = 16

FRAME_AXES = ("y", "zl", "x")
CLIP_AXES = ("zh", "core")

neg_fill = -1e30


def attend_kernel(order_ref, count_ref, q_ref, k_ref, v_ref, *rest, with_init, heads):
    if with_init:
        o0_ref, m0_ref, l0_ref, o_ref, m_ref, l_ref = rest
    else:
        o_ref, m_ref, l_ref = rest
    step = pl.program_id(0)

    @pl.when(step == 0)
    def _init():
        if with_init:
            m_ref[...] = m0_ref[...]
            l_ref[...] = l0_ref[...]
            o_ref[...] = o0_ref[...]
        else:
            m_ref[...] = jnp.full(m_ref.shape, neg_fill, jnp.float32)
            l_ref[...] = jnp.zeros(l_ref.shape, jnp.float32)
            o_ref[...] = jnp.zeros(o_ref.shape, jnp.float32)

    @pl.when(step < count_ref[0])
    def _slot():
        for head in range(heads):
            cols = pl.ds(head * HD, HD)
            scores = lax.dot_general(
                q_ref[:, cols], k_ref[0, 0, :, cols], (((1,), (1,)), ((), ())),
                preferred_element_type=jnp.float32,
            ) * (1.0 / math.sqrt(HD))
            running_max = m_ref[:, pl.ds(head * HD, 1)]
            new_max = jnp.maximum(running_max, jnp.max(scores, axis=1, keepdims=True))
            shrink = jnp.exp(running_max - new_max)
            weights = jnp.exp(scores - new_max)
            l_ref[:, cols] = l_ref[:, cols] * shrink + jnp.sum(weights, axis=1, keepdims=True)
            o_ref[:, cols] = o_ref[:, cols] * shrink + jnp.dot(
                weights.astype(jnp.bfloat16), v_ref[0, 0, :, cols],
                preferred_element_type=jnp.float32,
            )
            m_ref[:, cols] = jnp.broadcast_to(new_max, (new_max.shape[0], HD))


def attend(queries, arrived, order, count, init=None):
    tokens, width = queries.shape
    slots = arrived.shape[1]
    keys_each = arrived.shape[2]
    heads = width // HD
    with_init = init is not None

    def slot_at(s, order_ref, count_ref):
        return order_ref[jnp.clip(s, 0, jnp.maximum(count_ref[0] - 1, 0))]

    q_spec = pl.BlockSpec((tokens, width), lambda s, o, c: (0, 0))
    k_spec = pl.BlockSpec((1, 1, keys_each, width), lambda s, o, c: (0, slot_at(s, o, c), 0, 0))
    v_spec = pl.BlockSpec((1, 1, keys_each, width), lambda s, o, c: (1, slot_at(s, o, c), 0, 0))
    in_specs = [q_spec, k_spec, v_spec]
    operands = [queries, arrived, arrived]
    state_spec = pl.BlockSpec((tokens, width), lambda s, o, c: (0, 0))
    if with_init:
        in_specs += [state_spec] * 3
        operands += list(init)
    state_shape = jax.ShapeDtypeStruct((tokens, width), jnp.float32)
    return pl.pallas_call(
        lambda *refs: attend_kernel(*refs, with_init=with_init, heads=heads),
        grid_spec=pltpu.PrefetchScalarGridSpec(
            num_scalar_prefetch=2,
            grid=(slots,),
            in_specs=in_specs,
            out_specs=[state_spec] * 3,
        ),
        out_shape=[state_shape] * 3,
        compiler_params=pltpu.CompilerParams(dimension_semantics=("arbitrary",)),
        cost_estimate=pl.CostEstimate(
            flops=4 * slots * tokens * keys_each * width,
            transcendentals=slots * heads * tokens * keys_each,
            bytes_accessed=2 * slots * keys_each * width * 2 + 6 * tokens * width * 4,
        ),
    )(order, count, *operands)


def lookup(values_table, positions):
    table_width = values_table.shape[0]
    matches = positions[..., None] == jnp.arange(table_width, dtype=jnp.int32)
    return jnp.sum(jnp.where(matches, values_table, 0), axis=-1)


def pair_schedule(frames, slots, page_table, frame_lists, list_counts):
    max_slots = frame_lists.shape[1]
    dest = jnp.arange(frames, dtype=jnp.int32)[:, None]
    slot = jnp.arange(slots, dtype=jnp.int32)[None, :]
    even = dest - dest % 2
    combined = jnp.minimum((dest % 2) * slots + slot, max_slots)
    even_count = lookup(list_counts, even)
    for_even = combined < even_count
    listed_even = lookup(frame_lists.reshape(-1), even * max_slots + jnp.minimum(combined, max_slots - 1))
    listed_odd = lookup(
        frame_lists.reshape(-1),
        (even + 1) * max_slots + jnp.clip(combined - even_count, 0, max_slots - 1),
    )
    listed = jnp.where(for_even, listed_even, listed_odd)
    return lookup(page_table, (even // CF) * NC + listed)


def local(
    span_queries,
    span_keys,
    span_values,
    cache_keys,
    cache_values,
    page_table,
    frame_lists,
    list_counts,
    out_weight,
):
    frames = lax.axis_size(FRAME_AXES)
    own_frame = lax.axis_index(FRAME_AXES)
    tokens_here = span_queries.shape[1]
    row_width = span_queries.shape[2]
    heads_here = row_width // HD
    max_slots = frame_lists.shape[1]
    pair_blocks = max_slots + 1
    slots = (pair_blocks + 1) // 2
    own_queries = span_queries[0]
    own_keys = span_keys[0]
    own_values = span_values[0]

    weight = lax.all_gather(out_weight, ("zl", "x"), axis=1, tiled=True)

    blocks = pair_schedule(frames, slots, page_table, frame_lists, list_counts).T
    sent = jnp.stack([cache_keys[blocks], cache_values[blocks]], axis=0)
    arrived = lax.all_to_all(sent, FRAME_AXES, split_axis=2, concat_axis=2, tiled=True)
    arrived = arrived.reshape(2, slots, tokens_here, row_width)

    swap = [(i, i ^ 1) for i in range(lax.axis_size("x"))]
    partner_queries = lax.ppermute(own_queries, "x", swap)
    odd = own_frame % 2
    even_count = lookup(list_counts, own_frame - odd)
    other_count = jnp.where(
        odd == 0, jnp.maximum(0, slots - even_count), jnp.maximum(0, even_count - slots)
    )
    mine_count = jnp.where(
        odd == 0, jnp.minimum(even_count, slots), pair_blocks - jnp.maximum(even_count, slots)
    )
    step = jnp.arange(slots, dtype=jnp.int32)
    visit = jnp.where(odd == 0, slots - 1 - step, step)

    own_span = jnp.stack([own_keys, own_values])[:, None]
    own_start = attend(
        own_queries, own_span, jnp.zeros((1,), jnp.int32), jnp.ones((1,), jnp.int32)
    )
    weight, own_start = lax.optimization_barrier((weight, own_start))
    weight = lax.all_gather(weight, "y", axis=1, tiled=True)
    meet = jnp.abs(slots - even_count)
    before = jnp.clip(meet - other_count, 0, mine_count)
    after = mine_count - before

    def visits_from(first):
        at = jnp.minimum(step + first, slots - 1)
        return jnp.where(odd == 0, slots - 1 - at, at)

    other_state = attend(partner_queries, arrived, visit, other_count.reshape(1))
    own_state = attend(
        own_queries, arrived, visits_from(other_count), before.reshape(1), own_start
    )
    other_state, own_state = lax.optimization_barrier((other_state, own_state))
    other_out, other_max, other_sum = other_state
    got_max, got_sum, got_out = lax.ppermute(
        (other_max[:, ::HD], other_sum[:, ::HD], other_out), "x", swap
    )
    own_out, own_max, own_sum = attend(
        own_queries, arrived, visits_from(other_count + before), after.reshape(1), own_state
    )
    got_max = jnp.repeat(got_max, HD, axis=1)
    got_sum = jnp.repeat(got_sum, HD, axis=1)
    top = jnp.maximum(own_max, got_max)
    own_scale = jnp.exp(own_max - top)
    got_scale = jnp.exp(got_max - top)
    total_sum = own_sum * own_scale + got_sum * got_scale
    total_out = own_out * own_scale + got_out * got_scale
    attended = (total_out / total_sum).astype(jnp.bfloat16)
    partial_value = jnp.dot(attended, weight, preferred_element_type=jnp.float32)
    partial_value = partial_value.astype(jnp.bfloat16)
    quarters = lax.axis_size("zh") * lax.axis_size("core")
    quarter_rows = tokens_here // quarters
    chip_half = lax.axis_index("zh")
    core = lax.axis_index("core")
    cores = lax.axis_size("core")
    core_swap = [(i, cores - 1 - i) for i in range(cores)]

    def quarter(zh, k):
        return lax.dynamic_slice_in_dim(partial_value, (zh * cores + k) * quarter_rows, quarter_rows)

    theirs = quarter(1 - chip_half, core).astype(jnp.float32) + lax.ppermute(
        quarter(1 - chip_half, cores - 1 - core), "core", core_swap
    ).astype(jnp.float32)
    theirs = theirs.astype(jnp.bfloat16)
    ring = lax.axis_size("zh") * lax.axis_size("zl")
    z_axes = ("zh", "zl")

    def shifted(rows, by):
        return lax.ppermute(rows, z_axes, [(i, (i + by) % ring) for i in range(ring)])

    pieces = 2
    piece_rows = quarter_rows // pieces
    received = []
    for piece in range(pieces):
        rows = theirs[piece * piece_rows:(piece + 1) * piece_rows]
        first = 1 if piece < pieces // 2 else -1
        received.append(shifted(shifted(rows, first), first * (ring // 2 - 1)))
    received = jnp.concatenate(received, axis=0)
    mine = quarter(chip_half, core).astype(jnp.float32) + lax.ppermute(
        quarter(chip_half, cores - 1 - core), "core", core_swap
    ).astype(jnp.float32)
    own_rows = (mine + received.astype(jnp.float32)).astype(jnp.bfloat16)
    return own_rows[None]


def solution(mesh):
    frames = mesh.shape["fsdp"]
    fine = Mesh(
        np.asarray(mesh.devices).reshape(2, mesh.shape["clip"] // 2, frames // 16, 4, 4),
        CLIP_AXES + FRAME_AXES,
    )
    in_specs = (
        P(FRAME_AXES, None, CLIP_AXES),
        P(FRAME_AXES, None, CLIP_AXES),
        P(FRAME_AXES, None, CLIP_AXES),
        P(None, FRAME_AXES, CLIP_AXES),
        P(None, FRAME_AXES, CLIP_AXES),
        P(),
        P(),
        P(),
        P(CLIP_AXES, FRAME_AXES),
    )
    out_specs = P(FRAME_AXES, CLIP_AXES, None)
    return jax.shard_map(local, mesh=fine, in_specs=in_specs, out_specs=out_specs, check_vma=False)
```

```python
import math

import jax
import jax.numpy as jnp
import numpy as np
from jax import lax
from jax.experimental import pallas as pl
from jax.experimental.pallas import tpu as pltpu
from jax.sharding import Mesh
from jax.sharding import PartitionSpec as P

HD = 128
CF = 8
NC = 16

FRAME_AXES = ("y", "zl", "x")
CLIP_AXES = ("zh", "core")

neg_fill = -1e30


def attend_kernel(order_ref, count_ref, q_ref, k_ref, v_ref, *rest, with_init, heads):
    if with_init:
        o0_ref, m0_ref, l0_ref, o_ref, m_ref, l_ref = rest
    else:
        o_ref, m_ref, l_ref = rest
    step = pl.program_id(0)

    @pl.when(step == 0)
    def _init():
        if with_init:
            m_ref[...] = m0_ref[...]
            l_ref[...] = l0_ref[...]
            o_ref[...] = o0_ref[...]
        else:
            m_ref[...] = jnp.full(m_ref.shape, neg_fill, jnp.float32)
            l_ref[...] = jnp.zeros(l_ref.shape, jnp.float32)
            o_ref[...] = jnp.zeros(o_ref.shape, jnp.float32)

    @pl.when(step < count_ref[0])
    def _slot():
        def one_head(head, carry):
            cols = pl.ds(pl.multiple_of(head * HD, HD), HD)
            scores = lax.dot_general(
                q_ref[:, cols], k_ref[0, 0, :, cols], (((1,), (1,)), ((), ())),
                preferred_element_type=jnp.float32,
            ) * (1.0 / math.sqrt(HD))
            running_max = m_ref[:, cols][:, :1]
            new_max = jnp.maximum(running_max, jnp.max(scores, axis=1, keepdims=True))
            shrink = jnp.exp(running_max - new_max)
            weights = jnp.exp(scores - new_max)
            l_ref[:, cols] = l_ref[:, cols] * shrink + jnp.sum(weights, axis=1, keepdims=True)
            o_ref[:, cols] = o_ref[:, cols] * shrink + jnp.dot(
                weights.astype(jnp.bfloat16), v_ref[0, 0, :, cols],
                preferred_element_type=jnp.float32,
            )
            m_ref[:, cols] = jnp.broadcast_to(new_max, (new_max.shape[0], HD))
            return carry

        lax.fori_loop(0, heads, one_head, 0)


def attend(queries, arrived, order, count, init=None):
    tokens, width = queries.shape
    slots = arrived.shape[1]
    keys_each = arrived.shape[2]
    heads = width // HD
    with_init = init is not None

    def slot_at(s, order_ref, count_ref):
        return order_ref[jnp.clip(s, 0, jnp.maximum(count_ref[0] - 1, 0))]

    q_spec = pl.BlockSpec((tokens, width), lambda s, o, c: (0, 0))
    k_spec = pl.BlockSpec((1, 1, keys_each, width), lambda s, o, c: (0, slot_at(s, o, c), 0, 0))
    v_spec = pl.BlockSpec((1, 1, keys_each, width), lambda s, o, c: (1, slot_at(s, o, c), 0, 0))
    in_specs = [q_spec, k_spec, v_spec]
    operands = [queries, arrived, arrived]
    state_spec = pl.BlockSpec((tokens, width), lambda s, o, c: (0, 0))
    if with_init:
        in_specs += [state_spec] * 3
        operands += list(init)
    state_shape = jax.ShapeDtypeStruct((tokens, width), jnp.float32)
    return pl.pallas_call(
        lambda *refs: attend_kernel(*refs, with_init=with_init, heads=heads),
        grid_spec=pltpu.PrefetchScalarGridSpec(
            num_scalar_prefetch=2,
            grid=(slots,),
            in_specs=in_specs,
            out_specs=[state_spec] * 3,
        ),
        out_shape=[state_shape] * 3,
        compiler_params=pltpu.CompilerParams(dimension_semantics=("arbitrary",)),
        cost_estimate=pl.CostEstimate(
            flops=4 * slots * tokens * keys_each * width,
            transcendentals=slots * heads * tokens * keys_each,
            bytes_accessed=2 * slots * keys_each * width * 2 + 6 * tokens * width * 4,
        ),
    )(order, count, *operands)


def lookup(values_table, positions):
    table_width = values_table.shape[0]
    matches = positions[..., None] == jnp.arange(table_width, dtype=jnp.int32)
    return jnp.sum(jnp.where(matches, values_table, 0), axis=-1)


def pair_schedule(frames, slots, page_table, frame_lists, list_counts):
    max_slots = frame_lists.shape[1]
    dest = jnp.arange(frames, dtype=jnp.int32)[:, None]
    slot = jnp.arange(slots, dtype=jnp.int32)[None, :]
    even = dest - dest % 2
    combined = jnp.minimum((dest % 2) * slots + slot, max_slots)
    even_count = lookup(list_counts, even)
    for_even = combined < even_count
    listed_even = lookup(frame_lists.reshape(-1), even * max_slots + jnp.minimum(combined, max_slots - 1))
    listed_odd = lookup(
        frame_lists.reshape(-1),
        (even + 1) * max_slots + jnp.clip(combined - even_count, 0, max_slots - 1),
    )
    listed = jnp.where(for_even, listed_even, listed_odd)
    return lookup(page_table, (even // CF) * NC + listed)


def local(
    span_queries,
    span_keys,
    span_values,
    cache_keys,
    cache_values,
    page_table,
    frame_lists,
    list_counts,
    out_weight,
):
    frames = lax.axis_size(FRAME_AXES)
    own_frame = lax.axis_index(FRAME_AXES)
    tokens_here = span_queries.shape[1]
    row_width = span_queries.shape[2]
    heads_here = row_width // HD
    max_slots = frame_lists.shape[1]
    pair_blocks = max_slots + 1
    slots = (pair_blocks + 1) // 2
    own_queries = span_queries[0]
    own_keys = span_keys[0]
    own_values = span_values[0]

    weight = lax.all_gather(out_weight, ("zl", "x"), axis=1, tiled=True)

    blocks = pair_schedule(frames, slots, page_table, frame_lists, list_counts).T
    sent = jnp.stack([cache_keys[blocks], cache_values[blocks]], axis=0)
    arrived = lax.all_to_all(sent, FRAME_AXES, split_axis=2, concat_axis=2, tiled=True)
    arrived = arrived.reshape(2, slots, tokens_here, row_width)

    swap = [(i, i ^ 1) for i in range(lax.axis_size("x"))]
    partner_queries = lax.ppermute(own_queries, "x", swap)
    odd = own_frame % 2
    even_count = lookup(list_counts, own_frame - odd)
    other_count = jnp.where(
        odd == 0, jnp.maximum(0, slots - even_count), jnp.maximum(0, even_count - slots)
    )
    mine_count = jnp.where(
        odd == 0, jnp.minimum(even_count, slots), pair_blocks - jnp.maximum(even_count, slots)
    )
    step = jnp.arange(slots, dtype=jnp.int32)
    visit = jnp.where(odd == 0, slots - 1 - step, step)

    own_span = jnp.stack([own_keys, own_values])[:, None]
    own_start = attend(
        own_queries, own_span, jnp.zeros((1,), jnp.int32), jnp.ones((1,), jnp.int32)
    )
    weight, own_start = lax.optimization_barrier((weight, own_start))
    weight = lax.all_gather(weight, "y", axis=1, tiled=True)
    meet = jnp.abs(slots - even_count)
    before = jnp.clip(meet - other_count, 0, mine_count)
    after = mine_count - before

    def visits_from(first):
        at = jnp.minimum(step + first, slots - 1)
        return jnp.where(odd == 0, slots - 1 - at, at)

    other_state = attend(partner_queries, arrived, visit, other_count.reshape(1))
    own_state = attend(
        own_queries, arrived, visits_from(other_count), before.reshape(1), own_start
    )
    other_state, own_state = lax.optimization_barrier((other_state, own_state))
    other_out, other_max, other_sum = other_state
    got_max, got_sum, got_out = lax.ppermute(
        (other_max[:, ::HD], other_sum[:, ::HD], other_out), "x", swap
    )
    own_out, own_max, own_sum = attend(
        own_queries, arrived, visits_from(other_count + before), after.reshape(1), own_state
    )
    got_max = jnp.repeat(got_max, HD, axis=1)
    got_sum = jnp.repeat(got_sum, HD, axis=1)
    top = jnp.maximum(own_max, got_max)
    own_scale = jnp.exp(own_max - top)
    got_scale = jnp.exp(got_max - top)
    total_sum = own_sum * own_scale + got_sum * got_scale
    total_out = own_out * own_scale + got_out * got_scale
    attended = (total_out / total_sum).astype(jnp.bfloat16)
    partial_value = jnp.dot(attended, weight, preferred_element_type=jnp.float32)
    partial_value = partial_value.astype(jnp.bfloat16)
    quarters = lax.axis_size("zh") * lax.axis_size("core")
    quarter_rows = tokens_here // quarters
    chip_half = lax.axis_index("zh")
    core = lax.axis_index("core")
    cores = lax.axis_size("core")
    core_swap = [(i, cores - 1 - i) for i in range(cores)]

    def quarter(zh, k):
        return lax.dynamic_slice_in_dim(partial_value, (zh * cores + k) * quarter_rows, quarter_rows)

    theirs = quarter(1 - chip_half, core).astype(jnp.float32) + lax.ppermute(
        quarter(1 - chip_half, cores - 1 - core), "core", core_swap
    ).astype(jnp.float32)
    theirs = theirs.astype(jnp.bfloat16)
    ring = lax.axis_size("zh") * lax.axis_size("zl")
    z_axes = ("zh", "zl")

    def shifted(rows, by):
        return lax.ppermute(rows, z_axes, [(i, (i + by) % ring) for i in range(ring)])

    pieces = 2
    piece_rows = quarter_rows // pieces
    received = []
    for piece in range(pieces):
        rows = theirs[piece * piece_rows:(piece + 1) * piece_rows]
        first = 1 if piece < pieces // 2 else -1
        received.append(shifted(shifted(rows, first), first * (ring // 2 - 1)))
    received = jnp.concatenate(received, axis=0)
    mine = quarter(chip_half, core).astype(jnp.float32) + lax.ppermute(
        quarter(chip_half, cores - 1 - core), "core", core_swap
    ).astype(jnp.float32)
    own_rows = (mine + received.astype(jnp.float32)).astype(jnp.bfloat16)
    return own_rows[None]


def solution(mesh):
    frames = mesh.shape["fsdp"]
    fine = Mesh(
        np.asarray(mesh.devices).reshape(2, mesh.shape["clip"] // 2, frames // 16, 4, 4),
        CLIP_AXES + FRAME_AXES,
    )
    in_specs = (
        P(FRAME_AXES, None, CLIP_AXES),
        P(FRAME_AXES, None, CLIP_AXES),
        P(FRAME_AXES, None, CLIP_AXES),
        P(None, FRAME_AXES, CLIP_AXES),
        P(None, FRAME_AXES, CLIP_AXES),
        P(),
        P(),
        P(),
        P(CLIP_AXES, FRAME_AXES),
    )
    out_specs = P(FRAME_AXES, CLIP_AXES, None)
    return jax.shard_map(local, mesh=fine, in_specs=in_specs, out_specs=out_specs, check_vma=False)
```

```python
import math

import jax
import jax.numpy as jnp
import numpy as np
from jax import lax
from jax.experimental import pallas as pl
from jax.experimental.pallas import tpu as pltpu
from jax.sharding import Mesh
from jax.sharding import PartitionSpec as P

HD = 128
CF = 8
NC = 16

FRAME_AXES = ("y", "zl", "x")
CLIP_AXES = ("zh", "core")

neg_fill = -1e30


def attend_kernel(order_ref, count_ref, q_ref, k_ref, v_ref, *rest, with_init, heads):
    if with_init:
        o0_ref, m0_ref, l0_ref, o_ref, m_ref, l_ref = rest
    else:
        o_ref, m_ref, l_ref = rest
    step = pl.program_id(0)

    @pl.when(step == 0)
    def _init():
        if with_init:
            m_ref[...] = m0_ref[...]
            l_ref[...] = l0_ref[...]
            o_ref[...] = o0_ref[...]
        else:
            m_ref[...] = jnp.full(m_ref.shape, neg_fill, jnp.float32)
            l_ref[...] = jnp.zeros(l_ref.shape, jnp.float32)
            o_ref[...] = jnp.zeros(o_ref.shape, jnp.float32)

    @pl.when(step < count_ref[0])
    def _slot():
        def one_head(head, carry):
            cols = pl.ds(pl.multiple_of(head * HD, HD), HD)
            scores = lax.dot_general(
                q_ref[:, cols], k_ref[:, 0, 0, :, cols].reshape(-1, HD), (((1,), (1,)), ((), ())),
                preferred_element_type=jnp.float32,
            ) * (1.0 / math.sqrt(HD))
            running_max = m_ref[:, cols][:, :1]
            new_max = jnp.maximum(running_max, jnp.max(scores, axis=1, keepdims=True))
            shrink = jnp.exp(running_max - new_max)
            weights = jnp.exp(scores - new_max)
            l_ref[:, cols] = l_ref[:, cols] * shrink + jnp.sum(weights, axis=1, keepdims=True)
            o_ref[:, cols] = o_ref[:, cols] * shrink + jnp.dot(
                weights.astype(jnp.bfloat16), v_ref[:, 0, 0, :, cols].reshape(-1, HD),
                preferred_element_type=jnp.float32,
            )
            m_ref[:, cols] = jnp.broadcast_to(new_max, (new_max.shape[0], HD))
            return carry

        lax.fori_loop(0, heads, one_head, 0)


def attend(queries, arrived, order, count, init=None):
    tokens, width = queries.shape
    senders, _, slots, rows_each, _ = arrived.shape
    keys_each = senders * rows_each
    heads = width // HD
    with_init = init is not None

    def slot_at(s, order_ref, count_ref):
        return order_ref[jnp.clip(s, 0, jnp.maximum(count_ref[0] - 1, 0))]

    q_spec = pl.BlockSpec((tokens, width), lambda s, o, c: (0, 0))
    k_spec = pl.BlockSpec((senders, 1, 1, rows_each, width), lambda s, o, c: (0, 0, slot_at(s, o, c), 0, 0))
    v_spec = pl.BlockSpec((senders, 1, 1, rows_each, width), lambda s, o, c: (0, 1, slot_at(s, o, c), 0, 0))
    in_specs = [q_spec, k_spec, v_spec]
    operands = [queries, arrived, arrived]
    state_spec = pl.BlockSpec((tokens, width), lambda s, o, c: (0, 0))
    if with_init:
        in_specs += [state_spec] * 3
        operands += list(init)
    state_shape = jax.ShapeDtypeStruct((tokens, width), jnp.float32)
    return pl.pallas_call(
        lambda *refs: attend_kernel(*refs, with_init=with_init, heads=heads),
        grid_spec=pltpu.PrefetchScalarGridSpec(
            num_scalar_prefetch=2,
            grid=(slots,),
            in_specs=in_specs,
            out_specs=[state_spec] * 3,
        ),
        out_shape=[state_shape] * 3,
        compiler_params=pltpu.CompilerParams(dimension_semantics=("arbitrary",)),
        cost_estimate=pl.CostEstimate(
            flops=4 * slots * tokens * keys_each * width,
            transcendentals=slots * heads * tokens * keys_each,
            bytes_accessed=2 * slots * keys_each * width * 2 + 6 * tokens * width * 4,
        ),
    )(order, count, *operands)


def lookup(values_table, positions):
    table_width = values_table.shape[0]
    matches = positions[..., None] == jnp.arange(table_width, dtype=jnp.int32)
    return jnp.sum(jnp.where(matches, values_table, 0), axis=-1)


def pair_schedule(frames, slots, page_table, frame_lists, list_counts):
    max_slots = frame_lists.shape[1]
    dest = jnp.arange(frames, dtype=jnp.int32)[:, None]
    slot = jnp.arange(slots, dtype=jnp.int32)[None, :]
    even = dest - dest % 2
    combined = jnp.minimum((dest % 2) * slots + slot, max_slots)
    even_count = lookup(list_counts, even)
    for_even = combined < even_count
    listed_even = lookup(frame_lists.reshape(-1), even * max_slots + jnp.minimum(combined, max_slots - 1))
    listed_odd = lookup(
        frame_lists.reshape(-1),
        (even + 1) * max_slots + jnp.clip(combined - even_count, 0, max_slots - 1),
    )
    listed = jnp.where(for_even, listed_even, listed_odd)
    return lookup(page_table, (even // CF) * NC + listed)


def local(
    span_queries,
    span_keys,
    span_values,
    cache_keys,
    cache_values,
    page_table,
    frame_lists,
    list_counts,
    out_weight,
):
    frames = lax.axis_size(FRAME_AXES)
    own_frame = lax.axis_index(FRAME_AXES)
    tokens_here = span_queries.shape[1]
    row_width = span_queries.shape[2]
    heads_here = row_width // HD
    max_slots = frame_lists.shape[1]
    pair_blocks = max_slots + 1
    slots = (pair_blocks + 1) // 2
    own_queries = span_queries[0]
    own_keys = span_keys[0]
    own_values = span_values[0]

    weight = lax.all_gather(out_weight, ("zl", "x"), axis=1, tiled=True)

    blocks = pair_schedule(frames, slots, page_table, frame_lists, list_counts).T
    sent = jnp.stack([cache_keys[blocks.T], cache_values[blocks.T]], axis=1)
    arrived = lax.all_to_all(sent, FRAME_AXES, split_axis=0, concat_axis=0, tiled=True)

    swap = [(i, i ^ 1) for i in range(lax.axis_size("x"))]
    partner_queries = lax.ppermute(own_queries, "x", swap)
    odd = own_frame % 2
    even_count = lookup(list_counts, own_frame - odd)
    other_count = jnp.where(
        odd == 0, jnp.maximum(0, slots - even_count), jnp.maximum(0, even_count - slots)
    )
    mine_count = jnp.where(
        odd == 0, jnp.minimum(even_count, slots), pair_blocks - jnp.maximum(even_count, slots)
    )
    step = jnp.arange(slots, dtype=jnp.int32)
    visit = jnp.where(odd == 0, slots - 1 - step, step)

    own_span = jnp.stack([own_keys, own_values]).reshape(2, 1, -1, cache_keys.shape[1], row_width).transpose(2, 0, 1, 3, 4)
    own_start = attend(
        own_queries, own_span, jnp.zeros((1,), jnp.int32), jnp.ones((1,), jnp.int32)
    )
    weight, own_start = lax.optimization_barrier((weight, own_start))
    weight = lax.all_gather(weight, "y", axis=1, tiled=True)
    meet = jnp.abs(slots - even_count)
    before = jnp.clip(meet - other_count, 0, mine_count)
    after = mine_count - before

    def visits_from(first):
        at = jnp.minimum(step + first, slots - 1)
        return jnp.where(odd == 0, slots - 1 - at, at)

    other_state = attend(partner_queries, arrived, visit, other_count.reshape(1))
    own_state = attend(
        own_queries, arrived, visits_from(other_count), before.reshape(1), own_start
    )
    other_state, own_state = lax.optimization_barrier((other_state, own_state))
    other_out, other_max, other_sum = other_state
    got_max, got_sum, got_out = lax.ppermute(
        (other_max[:, ::HD], other_sum[:, ::HD], other_out), "x", swap
    )
    own_out, own_max, own_sum = attend(
        own_queries, arrived, visits_from(other_count + before), after.reshape(1), own_state
    )
    got_max = jnp.repeat(got_max, HD, axis=1)
    got_sum = jnp.repeat(got_sum, HD, axis=1)
    top = jnp.maximum(own_max, got_max)
    own_scale = jnp.exp(own_max - top)
    got_scale = jnp.exp(got_max - top)
    total_sum = own_sum * own_scale + got_sum * got_scale
    total_out = own_out * own_scale + got_out * got_scale
    attended = (total_out / total_sum).astype(jnp.bfloat16)
    partial_value = jnp.dot(attended, weight, preferred_element_type=jnp.float32)
    partial_value = partial_value.astype(jnp.bfloat16)
    quarters = lax.axis_size("zh") * lax.axis_size("core")
    quarter_rows = tokens_here // quarters
    chip_half = lax.axis_index("zh")
    core = lax.axis_index("core")
    cores = lax.axis_size("core")
    core_swap = [(i, cores - 1 - i) for i in range(cores)]

    def quarter(zh, k):
        return lax.dynamic_slice_in_dim(partial_value, (zh * cores + k) * quarter_rows, quarter_rows)

    theirs = quarter(1 - chip_half, core).astype(jnp.float32) + lax.ppermute(
        quarter(1 - chip_half, cores - 1 - core), "core", core_swap
    ).astype(jnp.float32)
    theirs = theirs.astype(jnp.bfloat16)
    ring = lax.axis_size("zh") * lax.axis_size("zl")
    z_axes = ("zh", "zl")

    def shifted(rows, by):
        return lax.ppermute(rows, z_axes, [(i, (i + by) % ring) for i in range(ring)])

    pieces = 2
    piece_rows = quarter_rows // pieces
    received = []
    for piece in range(pieces):
        rows = theirs[piece * piece_rows:(piece + 1) * piece_rows]
        first = 1 if piece < pieces // 2 else -1
        received.append(shifted(shifted(rows, first), first * (ring // 2 - 1)))
    received = jnp.concatenate(received, axis=0)
    mine = quarter(chip_half, core).astype(jnp.float32) + lax.ppermute(
        quarter(chip_half, cores - 1 - core), "core", core_swap
    ).astype(jnp.float32)
    own_rows = (mine + received.astype(jnp.float32)).astype(jnp.bfloat16)
    return own_rows[None]


def solution(mesh):
    frames = mesh.shape["fsdp"]
    fine = Mesh(
        np.asarray(mesh.devices).reshape(2, mesh.shape["clip"] // 2, frames // 16, 4, 4),
        CLIP_AXES + FRAME_AXES,
    )
    in_specs = (
        P(FRAME_AXES, None, CLIP_AXES),
        P(FRAME_AXES, None, CLIP_AXES),
        P(FRAME_AXES, None, CLIP_AXES),
        P(None, FRAME_AXES, CLIP_AXES),
        P(None, FRAME_AXES, CLIP_AXES),
        P(),
        P(),
        P(),
        P(CLIP_AXES, FRAME_AXES),
    )
    out_specs = P(FRAME_AXES, CLIP_AXES, None)
    return jax.shard_map(local, mesh=fine, in_specs=in_specs, out_specs=out_specs, check_vma=False)
```

```python
import math

import jax
import jax.numpy as jnp
import numpy as np
from jax import lax
from jax.experimental import pallas as pl
from jax.experimental.pallas import tpu as pltpu
from jax.sharding import Mesh
from jax.sharding import PartitionSpec as P

HD = 128
CF = 8
NC = 16

FRAME_AXES = ("y", "zl", "x")
CLIP_AXES = ("zh", "core")

neg_fill = -1e30


def attend_kernel(order_ref, count_ref, q_ref, k_ref, v_ref, *rest, with_init, heads):
    if with_init:
        o0_ref, m0_ref, l0_ref, o_ref, m_ref, l_ref = rest
    else:
        o_ref, m_ref, l_ref = rest
    step = pl.program_id(0)

    @pl.when(step == 0)
    def _init():
        if with_init:
            m_ref[...] = m0_ref[...]
            l_ref[...] = l0_ref[...]
            o_ref[...] = o0_ref[...]
        else:
            m_ref[...] = jnp.full(m_ref.shape, neg_fill, jnp.float32)
            l_ref[...] = jnp.zeros(l_ref.shape, jnp.float32)
            o_ref[...] = jnp.zeros(o_ref.shape, jnp.float32)

    @pl.when(step < count_ref[0])
    def _slot():
        def one_head(head, carry):
            cols = pl.ds(pl.multiple_of(head * HD, HD), HD)
            scores = lax.dot_general(
                q_ref[:, cols], k_ref[:, 0, 0, :, cols].reshape(-1, HD), (((1,), (1,)), ((), ())),
                preferred_element_type=jnp.float32,
            ) * (1.0 / math.sqrt(HD))
            running_max = m_ref[:, cols][:, :1]
            new_max = jnp.maximum(running_max, jnp.max(scores, axis=1, keepdims=True))
            shrink = jnp.exp(running_max - new_max)
            weights = jnp.exp(scores - new_max)
            l_ref[:, cols] = l_ref[:, cols] * shrink + jnp.sum(weights, axis=1, keepdims=True)
            o_ref[:, cols] = o_ref[:, cols] * shrink + jnp.dot(
                weights.astype(jnp.bfloat16), v_ref[:, 0, 0, :, cols].reshape(-1, HD),
                preferred_element_type=jnp.float32,
            )
            m_ref[:, cols] = jnp.broadcast_to(new_max, (new_max.shape[0], HD))
            return carry

        lax.fori_loop(0, heads, one_head, 0)


def attend(queries, arrived, order, count, init=None):
    tokens, width = queries.shape
    senders, _, slots, rows_each, _ = arrived.shape
    keys_each = senders * rows_each
    heads = width // HD
    with_init = init is not None

    def slot_at(s, order_ref, count_ref):
        return order_ref[jnp.clip(s, 0, jnp.maximum(count_ref[0] - 1, 0))]

    q_spec = pl.BlockSpec((tokens, width), lambda s, o, c: (0, 0))
    k_spec = pl.BlockSpec((senders, 1, 1, rows_each, width), lambda s, o, c: (0, 0, slot_at(s, o, c), 0, 0))
    v_spec = pl.BlockSpec((senders, 1, 1, rows_each, width), lambda s, o, c: (0, 1, slot_at(s, o, c), 0, 0))
    in_specs = [q_spec, k_spec, v_spec]
    operands = [queries, arrived, arrived]
    state_spec = pl.BlockSpec((tokens, width), lambda s, o, c: (0, 0))
    if with_init:
        in_specs += [state_spec] * 3
        operands += list(init)
    state_shape = jax.ShapeDtypeStruct((tokens, width), jnp.float32)
    return pl.pallas_call(
        lambda *refs: attend_kernel(*refs, with_init=with_init, heads=heads),
        grid_spec=pltpu.PrefetchScalarGridSpec(
            num_scalar_prefetch=2,
            grid=(slots,),
            in_specs=in_specs,
            out_specs=[state_spec] * 3,
        ),
        out_shape=[state_shape] * 3,
        compiler_params=pltpu.CompilerParams(dimension_semantics=("arbitrary",)),
        cost_estimate=pl.CostEstimate(
            flops=4 * slots * tokens * keys_each * width,
            transcendentals=slots * heads * tokens * keys_each,
            bytes_accessed=2 * slots * keys_each * width * 2 + 6 * tokens * width * 4,
        ),
    )(order, count, *operands)


def lookup(values_table, positions):
    table_width = values_table.shape[0]
    matches = positions[..., None] == jnp.arange(table_width, dtype=jnp.int32)
    return jnp.sum(jnp.where(matches, values_table, 0), axis=-1)


def pair_schedule(frames, slots, page_table, frame_lists, list_counts):
    max_slots = frame_lists.shape[1]
    dest = jnp.arange(frames, dtype=jnp.int32)[:, None]
    slot = jnp.arange(slots, dtype=jnp.int32)[None, :]
    even = dest - dest % 2
    combined = jnp.minimum((dest % 2) * slots + slot, max_slots)
    even_count = lookup(list_counts, even)
    for_even = combined < even_count
    listed_even = lookup(frame_lists.reshape(-1), even * max_slots + jnp.minimum(combined, max_slots - 1))
    listed_odd = lookup(
        frame_lists.reshape(-1),
        (even + 1) * max_slots + jnp.clip(combined - even_count, 0, max_slots - 1),
    )
    listed = jnp.where(for_even, listed_even, listed_odd)
    return lookup(page_table, (even // CF) * NC + listed)


def local(
    span_queries,
    span_keys,
    span_values,
    cache_keys,
    cache_values,
    page_table,
    frame_lists,
    list_counts,
    out_weight,
):
    frames = lax.axis_size(FRAME_AXES)
    own_frame = lax.axis_index(FRAME_AXES)
    tokens_here = span_queries.shape[1]
    row_width = span_queries.shape[2]
    heads_here = row_width // HD
    max_slots = frame_lists.shape[1]
    pair_blocks = max_slots + 1
    slots = (pair_blocks + 1) // 2
    own_queries = span_queries[0]
    own_keys = span_keys[0]
    own_values = span_values[0]

    weight = lax.all_gather(out_weight, ("zl", "x"), axis=1, tiled=True)

    blocks = pair_schedule(frames, slots, page_table, frame_lists, list_counts).T
    sent = jnp.stack([cache_keys[blocks.T], cache_values[blocks.T]], axis=1)
    arrived = lax.all_to_all(sent, FRAME_AXES, split_axis=0, concat_axis=0, tiled=True)

    swap = [(i, i ^ 1) for i in range(lax.axis_size("x"))]
    partner_queries = lax.ppermute(own_queries, "x", swap)
    odd = own_frame % 2
    even_count = lookup(list_counts, own_frame - odd)
    other_count = jnp.where(
        odd == 0, jnp.maximum(0, slots - even_count), jnp.maximum(0, even_count - slots)
    )
    mine_count = jnp.where(
        odd == 0, jnp.minimum(even_count, slots), pair_blocks - jnp.maximum(even_count, slots)
    )
    step = jnp.arange(slots, dtype=jnp.int32)
    visit = jnp.where(odd == 0, slots - 1 - step, step)

    own_span = jnp.stack([own_keys, own_values]).reshape(2, 1, -1, cache_keys.shape[1], row_width).transpose(2, 0, 1, 3, 4)
    own_start = attend(
        own_queries, own_span, jnp.zeros((1,), jnp.int32), jnp.ones((1,), jnp.int32)
    )
    weight, own_start = lax.optimization_barrier((weight, own_start))
    weight = lax.all_gather(weight, "y", axis=1, tiled=True)
    meet = jnp.abs(slots - even_count)
    before = jnp.clip(meet - other_count, 0, mine_count)
    after = mine_count - before

    def visits_from(first):
        at = jnp.minimum(step + first, slots - 1)
        return jnp.where(odd == 0, slots - 1 - at, at)

    other_state = attend(partner_queries, arrived, visit, other_count.reshape(1))
    own_state = attend(
        own_queries, arrived, visits_from(other_count), before.reshape(1), own_start
    )
    other_state, own_state = lax.optimization_barrier((other_state, own_state))
    other_out, other_max, other_sum = other_state
    other_mean = jnp.where(other_sum > 0, other_out / jnp.maximum(other_sum, 1e-30), 0.0)
    got_max, got_sum, got_mean = lax.ppermute(
        (other_max[:, ::HD], other_sum[:, ::HD], other_mean.astype(jnp.bfloat16)), "x", swap
    )
    own_out, own_max, own_sum = attend(
        own_queries, arrived, visits_from(other_count + before), after.reshape(1), own_state
    )
    got_max = jnp.repeat(got_max, HD, axis=1)
    got_sum = jnp.repeat(got_sum, HD, axis=1)
    got_out = got_mean.astype(jnp.float32) * got_sum
    top = jnp.maximum(own_max, got_max)
    own_scale = jnp.exp(own_max - top)
    got_scale = jnp.exp(got_max - top)
    total_sum = own_sum * own_scale + got_sum * got_scale
    total_out = own_out * own_scale + got_out * got_scale
    attended = (total_out / total_sum).astype(jnp.bfloat16)
    partial_value = jnp.dot(attended, weight, preferred_element_type=jnp.float32)
    partial_value = partial_value.astype(jnp.bfloat16)
    quarters = lax.axis_size("zh") * lax.axis_size("core")
    quarter_rows = tokens_here // quarters
    chip_half = lax.axis_index("zh")
    core = lax.axis_index("core")
    cores = lax.axis_size("core")
    core_swap = [(i, cores - 1 - i) for i in range(cores)]

    def quarter(zh, k):
        return lax.dynamic_slice_in_dim(partial_value, (zh * cores + k) * quarter_rows, quarter_rows)

    theirs = quarter(1 - chip_half, core).astype(jnp.float32) + lax.ppermute(
        quarter(1 - chip_half, cores - 1 - core), "core", core_swap
    ).astype(jnp.float32)
    theirs = theirs.astype(jnp.bfloat16)
    ring = lax.axis_size("zh") * lax.axis_size("zl")
    z_axes = ("zh", "zl")

    def shifted(rows, by):
        return lax.ppermute(rows, z_axes, [(i, (i + by) % ring) for i in range(ring)])

    pieces = 2
    piece_rows = quarter_rows // pieces
    received = []
    for piece in range(pieces):
        rows = theirs[piece * piece_rows:(piece + 1) * piece_rows]
        first = 1 if piece < pieces // 2 else -1
        received.append(shifted(shifted(rows, first), first * (ring // 2 - 1)))
    received = jnp.concatenate(received, axis=0)
    mine = quarter(chip_half, core).astype(jnp.float32) + lax.ppermute(
        quarter(chip_half, cores - 1 - core), "core", core_swap
    ).astype(jnp.float32)
    own_rows = (mine + received.astype(jnp.float32)).astype(jnp.bfloat16)
    return own_rows[None]


def solution(mesh):
    frames = mesh.shape["fsdp"]
    fine = Mesh(
        np.asarray(mesh.devices).reshape(2, mesh.shape["clip"] // 2, frames // 16, 4, 4),
        CLIP_AXES + FRAME_AXES,
    )
    in_specs = (
        P(FRAME_AXES, None, CLIP_AXES),
        P(FRAME_AXES, None, CLIP_AXES),
        P(FRAME_AXES, None, CLIP_AXES),
        P(None, FRAME_AXES, CLIP_AXES),
        P(None, FRAME_AXES, CLIP_AXES),
        P(),
        P(),
        P(),
        P(CLIP_AXES, FRAME_AXES),
    )
    out_specs = P(FRAME_AXES, CLIP_AXES, None)
    return jax.shard_map(local, mesh=fine, in_specs=in_specs, out_specs=out_specs, check_vma=False)
```

```python
import math

import jax
import jax.numpy as jnp
import numpy as np
from jax import lax
from jax.experimental import pallas as pl
from jax.experimental.pallas import tpu as pltpu
from jax.sharding import Mesh
from jax.sharding import PartitionSpec as P

HD = 128
CF = 8
NC = 16

FRAME_AXES = ("y", "zl", "x")
CLIP_AXES = ("zh", "core")

neg_fill = -1e30


def attend_kernel(order_ref, count_ref, q_ref, k_ref, v_ref, *rest, with_init, heads):
    if with_init:
        o0_ref, m0_ref, l0_ref, o_ref, m_ref, l_ref = rest
    else:
        o_ref, m_ref, l_ref = rest
    step = pl.program_id(0)

    @pl.when(step == 0)
    def _init():
        if with_init:
            m_ref[...] = m0_ref[...]
            l_ref[...] = l0_ref[...]
            o_ref[...] = o0_ref[...]
        else:
            m_ref[...] = jnp.full(m_ref.shape, neg_fill, jnp.float32)
            l_ref[...] = jnp.zeros(l_ref.shape, jnp.float32)
            o_ref[...] = jnp.zeros(o_ref.shape, jnp.float32)

    @pl.when(step < count_ref[0])
    def _slot():
        def one_head(head, carry):
            cols = pl.ds(pl.multiple_of(head * HD, HD), HD)
            scores = lax.dot_general(
                q_ref[:, cols], k_ref[:, 0, 0, :, cols].reshape(-1, HD), (((1,), (1,)), ((), ())),
                preferred_element_type=jnp.float32,
            ) * (1.0 / math.sqrt(HD))
            running_max = m_ref[:, cols][:, :1]
            new_max = jnp.maximum(running_max, jnp.max(scores, axis=1, keepdims=True))
            shrink = jnp.exp(running_max - new_max)
            weights = jnp.exp(scores - new_max)
            l_ref[:, cols] = l_ref[:, cols] * shrink + jnp.sum(weights, axis=1, keepdims=True)
            o_ref[:, cols] = o_ref[:, cols] * shrink + jnp.dot(
                weights.astype(jnp.bfloat16), v_ref[:, 0, 0, :, cols].reshape(-1, HD),
                preferred_element_type=jnp.float32,
            )
            m_ref[:, cols] = jnp.broadcast_to(new_max, (new_max.shape[0], HD))
            return carry

        lax.fori_loop(0, heads, one_head, 0)


def attend(queries, arrived, order, count, init=None):
    tokens, width = queries.shape
    senders, _, slots, rows_each, _ = arrived.shape
    keys_each = senders * rows_each
    heads = width // HD
    with_init = init is not None

    def slot_at(s, order_ref, count_ref):
        return order_ref[jnp.clip(s, 0, jnp.maximum(count_ref[0] - 1, 0))]

    q_spec = pl.BlockSpec((tokens, width), lambda s, o, c: (0, 0))
    k_spec = pl.BlockSpec((senders, 1, 1, rows_each, width), lambda s, o, c: (0, 0, slot_at(s, o, c), 0, 0))
    v_spec = pl.BlockSpec((senders, 1, 1, rows_each, width), lambda s, o, c: (0, 1, slot_at(s, o, c), 0, 0))
    in_specs = [q_spec, k_spec, v_spec]
    operands = [queries, arrived, arrived]
    state_spec = pl.BlockSpec((tokens, width), lambda s, o, c: (0, 0))
    if with_init:
        in_specs += [state_spec] * 3
        operands += list(init)
    state_shape = jax.ShapeDtypeStruct((tokens, width), jnp.float32)
    return pl.pallas_call(
        lambda *refs: attend_kernel(*refs, with_init=with_init, heads=heads),
        grid_spec=pltpu.PrefetchScalarGridSpec(
            num_scalar_prefetch=2,
            grid=(slots,),
            in_specs=in_specs,
            out_specs=[state_spec] * 3,
        ),
        out_shape=[state_shape] * 3,
        compiler_params=pltpu.CompilerParams(dimension_semantics=("arbitrary",)),
        cost_estimate=pl.CostEstimate(
            flops=4 * slots * tokens * keys_each * width,
            transcendentals=slots * heads * tokens * keys_each,
            bytes_accessed=2 * slots * keys_each * width * 2 + 6 * tokens * width * 4,
        ),
    )(order, count, *operands)


def lookup(values_table, positions):
    table_width = values_table.shape[0]
    matches = positions[..., None] == jnp.arange(table_width, dtype=jnp.int32)
    return jnp.sum(jnp.where(matches, values_table, 0), axis=-1)


def pair_schedule(frames, slots, page_table, frame_lists, list_counts):
    max_slots = frame_lists.shape[1]
    dest = jnp.arange(frames, dtype=jnp.int32)[:, None]
    slot = jnp.arange(slots, dtype=jnp.int32)[None, :]
    even = dest - dest % 2
    combined = jnp.minimum((dest % 2) * slots + slot, max_slots)
    even_count = lookup(list_counts, even)
    for_even = combined < even_count
    listed_even = lookup(frame_lists.reshape(-1), even * max_slots + jnp.minimum(combined, max_slots - 1))
    listed_odd = lookup(
        frame_lists.reshape(-1),
        (even + 1) * max_slots + jnp.clip(combined - even_count, 0, max_slots - 1),
    )
    listed = jnp.where(for_even, listed_even, listed_odd)
    return lookup(page_table, (even // CF) * NC + listed)


def local(
    span_queries,
    span_keys,
    span_values,
    cache_keys,
    cache_values,
    page_table,
    frame_lists,
    list_counts,
    out_weight,
):
    frames = lax.axis_size(FRAME_AXES)
    own_frame = lax.axis_index(FRAME_AXES)
    tokens_here = span_queries.shape[1]
    row_width = span_queries.shape[2]
    heads_here = row_width // HD
    max_slots = frame_lists.shape[1]
    pair_blocks = max_slots + 1
    slots = (pair_blocks + 1) // 2
    own_queries = span_queries[0]
    own_keys = span_keys[0]
    own_values = span_values[0]

    weight = lax.all_gather(out_weight, ("zl", "x"), axis=1, tiled=True)

    blocks = pair_schedule(frames, slots, page_table, frame_lists, list_counts).T
    sent = jnp.stack([cache_keys[blocks.T], cache_values[blocks.T]], axis=1)
    arrived = lax.all_to_all(sent, FRAME_AXES, split_axis=0, concat_axis=0, tiled=True)

    swap = [(i, i ^ 1) for i in range(lax.axis_size("x"))]
    partner_queries = lax.ppermute(own_queries, "x", swap)
    odd = own_frame % 2
    even_count = lookup(list_counts, own_frame - odd)
    other_count = jnp.where(
        odd == 0, jnp.maximum(0, slots - even_count), jnp.maximum(0, even_count - slots)
    )
    mine_count = jnp.where(
        odd == 0, jnp.minimum(even_count, slots), pair_blocks - jnp.maximum(even_count, slots)
    )
    step = jnp.arange(slots, dtype=jnp.int32)
    visit = jnp.where(odd == 0, slots - 1 - step, step)

    own_span = jnp.stack([own_keys, own_values]).reshape(2, 1, -1, cache_keys.shape[1], row_width).transpose(2, 0, 1, 3, 4)
    own_start = attend(
        own_queries, own_span, jnp.zeros((1,), jnp.int32), jnp.ones((1,), jnp.int32)
    )
    weight, own_start = lax.optimization_barrier((weight, own_start))
    weight = lax.all_gather(weight, "y", axis=1, tiled=True)
    meet = jnp.abs(slots - even_count)
    before = jnp.clip(meet - other_count, 0, mine_count)
    after = mine_count - before

    def visits_from(first):
        at = jnp.minimum(step + first, slots - 1)
        return jnp.where(odd == 0, slots - 1 - at, at)

    other_state = attend(partner_queries, arrived, visit, other_count.reshape(1))
    own_state = attend(
        own_queries, arrived, visits_from(other_count), before.reshape(1), own_start
    )
    other_state, own_state = lax.optimization_barrier((other_state, own_state))
    other_out, other_max, other_sum = other_state
    other_mean = jnp.where(other_sum > 0, other_out / jnp.maximum(other_sum, 1e-30), 0.0)
    got_stats, got_mean = lax.ppermute(
        (jnp.stack([other_max, other_sum])[:, :, ::HD], other_mean.astype(jnp.bfloat16)), "x", swap
    )
    got_max, got_sum = got_stats[0], got_stats[1]
    own_out, own_max, own_sum = attend(
        own_queries, arrived, visits_from(other_count + before), after.reshape(1), own_state
    )
    got_max = jnp.repeat(got_max, HD, axis=1)
    got_sum = jnp.repeat(got_sum, HD, axis=1)
    got_out = got_mean.astype(jnp.float32) * got_sum
    top = jnp.maximum(own_max, got_max)
    own_scale = jnp.exp(own_max - top)
    got_scale = jnp.exp(got_max - top)
    total_sum = own_sum * own_scale + got_sum * got_scale
    total_out = own_out * own_scale + got_out * got_scale
    attended = (total_out / total_sum).astype(jnp.bfloat16)
    partial_value = jnp.dot(attended, weight, preferred_element_type=jnp.float32)
    partial_value = partial_value.astype(jnp.bfloat16)
    quarters = lax.axis_size("zh") * lax.axis_size("core")
    quarter_rows = tokens_here // quarters
    chip_half = lax.axis_index("zh")
    core = lax.axis_index("core")
    cores = lax.axis_size("core")
    core_swap = [(i, cores - 1 - i) for i in range(cores)]

    def quarter(zh, k):
        return lax.dynamic_slice_in_dim(partial_value, (zh * cores + k) * quarter_rows, quarter_rows)

    theirs = quarter(1 - chip_half, core).astype(jnp.float32) + lax.ppermute(
        quarter(1 - chip_half, cores - 1 - core), "core", core_swap
    ).astype(jnp.float32)
    theirs = theirs.astype(jnp.bfloat16)
    ring = lax.axis_size("zh") * lax.axis_size("zl")
    z_axes = ("zh", "zl")

    def shifted(rows, by):
        return lax.ppermute(rows, z_axes, [(i, (i + by) % ring) for i in range(ring)])

    pieces = 2
    piece_rows = quarter_rows // pieces
    received = []
    for piece in range(pieces):
        rows = theirs[piece * piece_rows:(piece + 1) * piece_rows]
        first = 1 if piece < pieces // 2 else -1
        received.append(shifted(shifted(rows, first), first * (ring // 2 - 1)))
    received = jnp.concatenate(received, axis=0)
    mine = quarter(chip_half, core).astype(jnp.float32) + lax.ppermute(
        quarter(chip_half, cores - 1 - core), "core", core_swap
    ).astype(jnp.float32)
    own_rows = (mine + received.astype(jnp.float32)).astype(jnp.bfloat16)
    return own_rows[None]


def solution(mesh):
    frames = mesh.shape["fsdp"]
    fine = Mesh(
        np.asarray(mesh.devices).reshape(2, mesh.shape["clip"] // 2, frames // 16, 4, 4),
        CLIP_AXES + FRAME_AXES,
    )
    in_specs = (
        P(FRAME_AXES, None, CLIP_AXES),
        P(FRAME_AXES, None, CLIP_AXES),
        P(FRAME_AXES, None, CLIP_AXES),
        P(None, FRAME_AXES, CLIP_AXES),
        P(None, FRAME_AXES, CLIP_AXES),
        P(),
        P(),
        P(),
        P(CLIP_AXES, FRAME_AXES),
    )
    out_specs = P(FRAME_AXES, CLIP_AXES, None)
    return jax.shard_map(local, mesh=fine, in_specs=in_specs, out_specs=out_specs, check_vma=False)
```
